32 devices in a mesh: seq: 4 (over y, x), tp: 8 (over z, core).
Axes of the slice: x: 2, y: 2, z: 4, core: 2. Of those that a mesh axis runs over, the one named last changes fastest.
Arguments:
- hidden: bfloat16 [512, 28672], P('seq', 'tp'), may hold values from -6 to 6
- down_weight: bfloat16 [28672, 8192], P('tp', 'seq'), may hold values from -0.03125 to 0.03125
- channel_scale: float32 [8192], P('seq'), may hold values from 0.25 to 1.75
Outputs:
- mixed: bfloat16 [512, 8192], P('tp', 'seq')
The draws below stay inside these ranges and needn't reach their ends.
All inputs are finite; a program needn't handle non-finite values.
Results may differ from the reference program's by a relative error of at most 0.0049.
Values may be sent and summed in bfloat16 or wider, within the bound.
No kernel may reach another device: no remote copies, remote signals or barrier semaphores. Data moves between devices by JAX's collectives and lax.ppermute only.
A program may use at most 128 MiB of HBM per device.

```python
import math
import jax
import jax.numpy as jnp
import numpy as np
from jax import lax

D = 8192
WALSH = 1024
PALEY = 28
FF = 28672
TOKENS = 512


def block_scale(stream_key, dims, pieces, smallest, top_value):
    factor_of = 1.0
    for position, parts in pieces:
        heights = jax.random.uniform(jax.random.fold_in(jax.random.fold_in(stream_key, 6), position), (parts,), jnp.float32, smallest / len(pieces), top_value / len(pieces))
        factor_of = factor_of * jnp.repeat(jnp.exp(heights), dims[position] // parts).reshape((-1,) + (1,) * (len(dims) - 1 - position))
    return factor_of


def noise(own_key, extent, deviation, reach, shards=(), kind=jnp.bfloat16):
    values = deviation * jax.random.normal(own_key, extent, jnp.float32)
    if shards:
        values = values * block_scale(own_key, extent, shards, -0.22, 0.18)
    return jnp.clip(values, -reach, reach).astype(kind)


def setup_inputs(seed: int = 0) -> dict:
    seeds = jax.random.split(jax.random.key(seed), 4)
    return {
        "hidden": noise(seeds[0], (TOKENS, FF), 1.0, 6.0, ((0, 4), (1, 8))),
        "down_weight": noise(seeds[1], (FF, D), FF ** -0.5, 0.03125, ((0, 8), (1, 4))),
        "channel_scale": jnp.clip(1.0 + 0.15 * jax.random.normal(seeds[2], (D,), jnp.float32), 0.25, 1.75),
    }


def paley_table():
    residues = set((value * value % 13 for value in range(1, 13)))
    conference = np.zeros((14, 14))
    conference[0, 1:] = 1.0
    conference[1:, 0] = 1.0
    for first in range(13):
        for second in range(13):
            gap = (second - first) % 13
            if gap != 0:
                conference[1 + first, 1 + second] = 1.0 if gap in residues else -1.0
    upper = np.array([[1.0, 1.0], [1.0, -1.0]])
    lower = np.array([[1.0, -1.0], [-1.0, -1.0]])
    return np.kron(conference, upper) + np.kron(np.eye(14), lower)

def reference(hidden, down_weight, channel_scale):
    row_count = hidden.shape[0]
    values = hidden.astype(jnp.float32).reshape(row_count, WALSH, PALEY)
    table = jnp.asarray(paley_table(), jnp.float32)
    values = jnp.einsum('rba,ac->rbc', values, table, precision=lax.Precision.HIGHEST)
    stride = 1
    while stride < WALSH:
        paired = values.reshape(row_count, WALSH // (2 * stride), 2, stride, PALEY)
        values = jnp.stack([paired[:, :, 0] + paired[:, :, 1], paired[:, :, 0] - paired[:, :, 1]], axis=2)
        values = values.reshape(row_count, WALSH, PALEY)
        stride = stride * 2
    rotated = (values.reshape(row_count, FF) * (1.0 / math.sqrt(FF))).astype(jnp.bfloat16)
    product = jnp.dot(rotated, down_weight, preferred_element_type=jnp.float32)
    return (product * channel_scale[None, :]).astype(jnp.bfloat16)
```

```python
import math

import jax
import jax.numpy as jnp
import numpy as np
from jax import lax
from jax.sharding import PartitionSpec as P

PALEY = 28
INNER = 32


def paley_table():
    residues = set((value * value % 13 for value in range(1, 13)))
    conference = np.zeros((14, 14))
    conference[0, 1:] = 1.0
    conference[1:, 0] = 1.0
    for first in range(13):
        for second in range(13):
            gap = (second - first) % 13
            if gap != 0:
                conference[1 + first, 1 + second] = 1.0 if gap in residues else -1.0
    upper = np.array([[1.0, 1.0], [1.0, -1.0]])
    lower = np.array([[1.0, -1.0], [-1.0, -1.0]])
    return np.kron(conference, upper) + np.kron(np.eye(14), lower)


def walsh_table(order):
    index_rows = np.arange(order)[:, None]
    index_cols = np.arange(order)[None, :]
    signs = np.ones((order, order))
    bit_value = 1
    while bit_value < order:
        both_set = index_rows // bit_value % 2 * (index_cols // bit_value % 2)
        signs = signs * (1 - 2 * both_set)
        bit_value = bit_value * 2
    return signs


def rotate(spread):
    rows, total_units = spread.shape
    walsh = total_units // PALEY
    outer_order = walsh // INNER
    width = INNER * PALEY
    inner_table = jnp.asarray(np.kron(walsh_table(INNER), paley_table()), jnp.bfloat16)
    outer_table = jnp.asarray(walsh_table(outer_order), jnp.float32)
    blocks = spread.reshape(rows, outer_order, width)
    inner = jnp.einsum("rbl,lm->rbm", blocks, inner_table, preferred_element_type=jnp.float32)
    outer = jnp.einsum("rbm,bc->rcm", inner, outer_table, precision=lax.Precision.HIGHEST)
    factor = 1.0 / math.sqrt(total_units)
    return (outer * factor).astype(jnp.bfloat16).reshape(rows, total_units)


def shards(hidden, down_weight, channel_scale):
    spread = lax.all_to_all(hidden, "tp", split_axis=0, concat_axis=1, tiled=True)
    turned = rotate(spread)
    rotated = lax.all_to_all(turned, "tp", split_axis=1, concat_axis=0, tiled=True)
    partial_terms = jnp.dot(
        lax.all_gather(rotated, "seq", axis=0, tiled=True),
        down_weight,
        preferred_element_type=jnp.float32,
    )
    summed = lax.psum_scatter(
        partial_terms.astype(jnp.bfloat16), "tp", scatter_dimension=0, tiled=True
    )
    return (summed.astype(jnp.float32) * channel_scale[None, :]).astype(jnp.bfloat16)


def solution(mesh):
    placed = (P("seq", "tp"), P("tp", "seq"), P("seq"))
    return jax.shard_map(
        shards, mesh=mesh, in_specs=placed, out_specs=P("tp", "seq"), check_vma=False
    )
```

```python
import math

import jax
import jax.numpy as jnp
import numpy as np
from jax import lax
from jax.sharding import PartitionSpec as P

PALEY = 28
INNER = 32
CHUNKS = 2


def paley_table():
    residues = set((value * value % 13 for value in range(1, 13)))
    conference = np.zeros((14, 14))
    conference[0, 1:] = 1.0
    conference[1:, 0] = 1.0
    for first in range(13):
        for second in range(13):
            gap = (second - first) % 13
            if gap != 0:
                conference[1 + first, 1 + second] = 1.0 if gap in residues else -1.0
    upper = np.array([[1.0, 1.0], [1.0, -1.0]])
    lower = np.array([[1.0, -1.0], [-1.0, -1.0]])
    return np.kron(conference, upper) + np.kron(np.eye(14), lower)


def walsh_table(order):
    index_rows = np.arange(order)[:, None]
    index_cols = np.arange(order)[None, :]
    signs = np.ones((order, order))
    bit_value = 1
    while bit_value < order:
        both_set = index_rows // bit_value % 2 * (index_cols // bit_value % 2)
        signs = signs * (1 - 2 * both_set)
        bit_value = bit_value * 2
    return signs


def rotate(spread):
    rows, total_units = spread.shape
    walsh = total_units // PALEY
    outer_order = walsh // INNER
    width = INNER * PALEY
    inner_table = jnp.asarray(np.kron(walsh_table(INNER), paley_table()), jnp.bfloat16)
    outer_table = jnp.asarray(walsh_table(outer_order), jnp.float32)
    blocks = spread.reshape(rows, outer_order, width)
    inner = jnp.einsum("rbl,lm->rbm", blocks, inner_table, preferred_element_type=jnp.float32)
    outer = jnp.einsum("rbm,bc->rcm", inner, outer_table, precision=lax.Precision.HIGHEST)
    factor = 1.0 / math.sqrt(total_units)
    return (outer * factor).astype(jnp.bfloat16).reshape(rows, total_units)


def shards(hidden, down_weight, channel_scale):
    seq_count = lax.axis_size("seq")
    tp_count = lax.axis_size("tp")
    tokens, units = hidden.shape
    groups = tp_count // seq_count
    owned = tokens // groups
    piece = owned // CHUNKS
    grouped = hidden.reshape(groups, CHUNKS, piece, units)
    outputs = []
    for chunk in range(CHUNKS):
        part = grouped[:, chunk].reshape(groups * piece, units)
        spread = lax.all_to_all(part, "tp", split_axis=0, concat_axis=1, tiled=True)
        turned = rotate(spread)
        rotated = lax.all_to_all(turned, "tp", split_axis=1, concat_axis=0, tiled=True)
        partial_terms = jnp.dot(
            lax.all_gather(rotated, "seq", axis=0, tiled=True),
            down_weight,
            preferred_element_type=jnp.float32,
        )
        outputs.append(lax.psum_scatter(partial_terms, "tp", scatter_dimension=0, tiled=True))
    summed = jnp.concatenate(outputs, axis=0)
    return (summed * channel_scale[None, :]).astype(jnp.bfloat16)


def solution(mesh):
    placed = (P("seq", "tp"), P("tp", "seq"), P("seq"))
    return jax.shard_map(
        shards, mesh=mesh, in_specs=placed, out_specs=P("tp", "seq"), check_vma=False
    )
```

```python
import math

import jax
import jax.numpy as jnp
import numpy as np
from jax import lax
from jax.sharding import PartitionSpec as P

PALEY = 28
INNER = 32
CHUNKS = 1


def paley_table():
    residues = set((value * value % 13 for value in range(1, 13)))
    conference = np.zeros((14, 14))
    conference[0, 1:] = 1.0
    conference[1:, 0] = 1.0
    for first in range(13):
        for second in range(13):
            gap = (second - first) % 13
            if gap != 0:
                conference[1 + first, 1 + second] = 1.0 if gap in residues else -1.0
    upper = np.array([[1.0, 1.0], [1.0, -1.0]])
    lower = np.array([[1.0, -1.0], [-1.0, -1.0]])
    return np.kron(conference, upper) + np.kron(np.eye(14), lower)


def walsh_table(order):
    index_rows = np.arange(order)[:, None]
    index_cols = np.arange(order)[None, :]
    signs = np.ones((order, order))
    bit_value = 1
    while bit_value < order:
        both_set = index_rows // bit_value % 2 * (index_cols // bit_value % 2)
        signs = signs * (1 - 2 * both_set)
        bit_value = bit_value * 2
    return signs


def rotate(spread):
    rows, total_units = spread.shape
    walsh = total_units // PALEY
    outer_order = walsh // INNER
    width = INNER * PALEY
    inner_table = jnp.asarray(np.kron(walsh_table(INNER), paley_table()), jnp.bfloat16)
    outer_table = jnp.asarray(walsh_table(outer_order), jnp.float32)
    blocks = spread.reshape(rows, outer_order, width)
    inner = jnp.einsum("rbl,lm->rbm", blocks, inner_table, preferred_element_type=jnp.float32)
    outer = jnp.einsum("rbm,bc->rcm", inner, outer_table, precision=lax.Precision.HIGHEST)
    factor = 1.0 / math.sqrt(total_units)
    return (outer * factor).astype(jnp.bfloat16).reshape(rows, total_units)


def gather_seq(block):
    seq_count = lax.axis_size("seq")
    if seq_count != 4:
        return lax.all_gather(block, "seq", axis=0, tiled=True)
    rows = block.shape[0]
    half = rows // 2
    across_x = lax.ppermute(block, "seq", [(s, s ^ 1) for s in range(4)])
    across_y = lax.ppermute(block, "seq", [(s, s ^ 2) for s in range(4)])
    first = lax.ppermute(across_y[:half], "seq", [(s, s ^ 1) for s in range(4)])
    second = lax.ppermute(across_x[half:], "seq", [(s, s ^ 2) for s in range(4)])
    diagonal = jnp.concatenate([first, second], axis=0)
    stacked = jnp.stack([block, across_x, across_y, diagonal])
    me = lax.axis_index("seq")
    return jnp.concatenate(
        [lax.dynamic_index_in_dim(stacked, me ^ other, 0, keepdims=False) for other in range(4)],
        axis=0,
    )


def shards(hidden, down_weight, channel_scale):
    seq_count = lax.axis_size("seq")
    tp_count = lax.axis_size("tp")
    tokens, units = hidden.shape
    groups = tp_count // seq_count
    owned = tokens // groups
    piece = owned // CHUNKS
    grouped = hidden.reshape(groups, CHUNKS, piece, units)
    outputs = []
    for chunk in range(CHUNKS):
        part = grouped[:, chunk].reshape(groups * piece, units)
        spread = lax.all_to_all(part, "tp", split_axis=0, concat_axis=1, tiled=True)
        turned = rotate(spread)
        rotated = lax.all_to_all(turned, "tp", split_axis=1, concat_axis=0, tiled=True)
        partial_terms = jnp.dot(
            gather_seq(rotated), down_weight, preferred_element_type=jnp.float32
        )
        outputs.append(lax.psum_scatter(partial_terms, "tp", scatter_dimension=0, tiled=True))
    summed = jnp.concatenate(outputs, axis=0)
    return (summed * channel_scale[None, :]).astype(jnp.bfloat16)


def solution(mesh):
    placed = (P("seq", "tp"), P("tp", "seq"), P("seq"))
    return jax.shard_map(
        shards, mesh=mesh, in_specs=placed, out_specs=P("tp", "seq"), check_vma=False
    )
```

```python
import math

import jax
import jax.numpy as jnp
import numpy as np
from jax import lax
from jax.sharding import PartitionSpec as P

PALEY = 28
INNER = 32
CHUNKS = 1


def paley_table():
    residues = set((value * value % 13 for value in range(1, 13)))
    conference = np.zeros((14, 14))
    conference[0, 1:] = 1.0
    conference[1:, 0] = 1.0
    for first in range(13):
        for second in range(13):
            gap = (second - first) % 13
            if gap != 0:
                conference[1 + first, 1 + second] = 1.0 if gap in residues else -1.0
    upper = np.array([[1.0, 1.0], [1.0, -1.0]])
    lower = np.array([[1.0, -1.0], [-1.0, -1.0]])
    return np.kron(conference, upper) + np.kron(np.eye(14), lower)


def walsh_table(order):
    index_rows = np.arange(order)[:, None]
    index_cols = np.arange(order)[None, :]
    signs = np.ones((order, order))
    bit_value = 1
    while bit_value < order:
        both_set = index_rows // bit_value % 2 * (index_cols // bit_value % 2)
        signs = signs * (1 - 2 * both_set)
        bit_value = bit_value * 2
    return signs


def rotate(spread):
    rows, total_units = spread.shape
    walsh = total_units // PALEY
    outer_order = walsh // INNER
    width = INNER * PALEY
    inner_table = jnp.asarray(np.kron(walsh_table(INNER), paley_table()), jnp.bfloat16)
    outer_table = jnp.asarray(walsh_table(outer_order), jnp.float32)
    blocks = spread.reshape(rows, outer_order, width)
    inner = jnp.einsum("rbl,lm->rbm", blocks, inner_table, preferred_element_type=jnp.float32)
    outer = jnp.einsum("rbm,bc->rcm", inner, outer_table, precision=lax.Precision.HIGHEST)
    factor = 1.0 / math.sqrt(total_units)
    return (outer * factor).astype(jnp.bfloat16).reshape(rows, total_units)


def gathered_product(block, down_weight):
    seq_count = lax.axis_size("seq")
    if seq_count != 4:
        gathered = lax.all_gather(block, "seq", axis=0, tiled=True)
        return jnp.dot(gathered, down_weight, preferred_element_type=jnp.float32)
    rows = block.shape[0]
    half = rows // 2
    across_x = lax.ppermute(block, "seq", [(s, s ^ 1) for s in range(4)])
    across_y = lax.ppermute(block, "seq", [(s, s ^ 2) for s in range(4)])
    first = lax.ppermute(across_y[:half], "seq", [(s, s ^ 1) for s in range(4)])
    second = lax.ppermute(across_x[half:], "seq", [(s, s ^ 2) for s in range(4)])
    diagonal = jnp.concatenate([first, second], axis=0)
    me = lax.axis_index("seq")
    columns = down_weight.shape[1]
    result = jnp.zeros((4 * rows, columns), jnp.float32)
    for other, piece in enumerate((block, across_x, across_y, diagonal)):
        product = jnp.dot(piece, down_weight, preferred_element_type=jnp.float32)
        result = lax.dynamic_update_slice_in_dim(result, product, (me ^ other) * rows, 0)
    return result


def shards(hidden, down_weight, channel_scale):
    seq_count = lax.axis_size("seq")
    tp_count = lax.axis_size("tp")
    tokens, units = hidden.shape
    groups = tp_count // seq_count
    owned = tokens // groups
    piece = owned // CHUNKS
    grouped = hidden.reshape(groups, CHUNKS, piece, units)
    outputs = []
    for chunk in range(CHUNKS):
        part = grouped[:, chunk].reshape(groups * piece, units)
        spread = lax.all_to_all(part, "tp", split_axis=0, concat_axis=1, tiled=True)
        turned = rotate(spread)
        rotated = lax.all_to_all(turned, "tp", split_axis=1, concat_axis=0, tiled=True)
        partial_terms = gathered_product(rotated, down_weight)
        outputs.append(lax.psum_scatter(partial_terms, "tp", scatter_dimension=0, tiled=True))
    summed = jnp.concatenate(outputs, axis=0)
    return (summed * channel_scale[None, :]).astype(jnp.bfloat16)


def solution(mesh):
    placed = (P("seq", "tp"), P("tp", "seq"), P("seq"))
    return jax.shard_map(
        shards, mesh=mesh, in_specs=placed, out_specs=P("tp", "seq"), check_vma=False
    )
```

```python
import math

import jax
import jax.numpy as jnp
import numpy as np
from jax import lax
from jax.sharding import PartitionSpec as P

PALEY = 28
INNER = 32
CHUNKS = 1


def paley_table():
    residues = set((value * value % 13 for value in range(1, 13)))
    conference = np.zeros((14, 14))
    conference[0, 1:] = 1.0
    conference[1:, 0] = 1.0
    for first in range(13):
        for second in range(13):
            gap = (second - first) % 13
            if gap != 0:
                conference[1 + first, 1 + second] = 1.0 if gap in residues else -1.0
    upper = np.array([[1.0, 1.0], [1.0, -1.0]])
    lower = np.array([[1.0, -1.0], [-1.0, -1.0]])
    return np.kron(conference, upper) + np.kron(np.eye(14), lower)


def inner_kron():
    walsh = jnp.asarray(walsh_table(INNER), jnp.bfloat16)
    paley = jnp.asarray(paley_table(), jnp.bfloat16)
    width = INNER * PALEY
    return (walsh[:, None, :, None] * paley[None, :, None, :]).reshape(width, width)


def walsh_table(order):
    index_rows = np.arange(order)[:, None]
    index_cols = np.arange(order)[None, :]
    signs = np.ones((order, order))
    bit_value = 1
    while bit_value < order:
        both_set = index_rows // bit_value % 2 * (index_cols // bit_value % 2)
        signs = signs * (1 - 2 * both_set)
        bit_value = bit_value * 2
    return signs


def rotate(spread):
    rows, total_units = spread.shape
    walsh = total_units // PALEY
    outer_order = walsh // INNER
    width = INNER * PALEY
    inner_table = inner_kron()
    outer_table = jnp.asarray(walsh_table(outer_order), jnp.float32)
    blocks = spread.reshape(rows, outer_order, width)
    inner = jnp.einsum("rbl,lm->rbm", blocks, inner_table, preferred_element_type=jnp.float32)
    outer = jnp.einsum("rbm,bc->rcm", inner, outer_table, precision=lax.Precision.HIGHEST)
    factor = 1.0 / math.sqrt(total_units)
    return (outer * factor).astype(jnp.bfloat16).reshape(rows, total_units)


def gathered_product(block, down_weight):
    seq_count = lax.axis_size("seq")
    if seq_count != 4:
        gathered = lax.all_gather(block, "seq", axis=0, tiled=True)
        return jnp.dot(gathered, down_weight, preferred_element_type=jnp.float32)
    rows = block.shape[0]
    half = rows // 2
    across_x = lax.ppermute(block, "seq", [(s, s ^ 1) for s in range(4)])
    across_y = lax.ppermute(block, "seq", [(s, s ^ 2) for s in range(4)])
    first = lax.ppermute(across_y[:half], "seq", [(s, s ^ 1) for s in range(4)])
    second = lax.ppermute(across_x[half:], "seq", [(s, s ^ 2) for s in range(4)])
    diagonal = jnp.concatenate([first, second], axis=0)
    me = lax.axis_index("seq")
    columns = down_weight.shape[1]
    result = jnp.zeros((4 * rows, columns), jnp.float32)
    for other, piece in enumerate((block, across_x, across_y, diagonal)):
        product = jnp.dot(piece, down_weight, preferred_element_type=jnp.float32)
        result = lax.dynamic_update_slice_in_dim(result, product, (me ^ other) * rows, 0)
    return result


def spread_rotate_return(part):
    tp_count = lax.axis_size("tp")
    rows, units = part.shape
    share = rows // tp_count
    width = INNER * PALEY
    sub = units // width
    me = lax.axis_index("tp")
    pairs = lambda distance: [(k, k ^ distance) for k in range(tp_count)]
    inner_table = inner_kron()
    landed = []
    for distance in range(tp_count):
        send = lax.dynamic_slice_in_dim(part, (me ^ distance) * share, share, 0)
        if distance:
            send = lax.ppermute(send, "tp", pairs(distance))
        landed.append(
            jnp.einsum(
                "rbl,lm->rbm",
                send.reshape(share, sub, width),
                inner_table,
                preferred_element_type=jnp.float32,
            )
        )
    inner = jnp.stack(landed, axis=1).reshape(share, tp_count * sub, width)
    order = jnp.arange(tp_count, dtype=jnp.int32)
    source = me ^ order
    signs = 1 - 2 * (lax.population_count(source[:, None] & source[None, :]) % 2)
    mixing = jnp.kron(signs.astype(jnp.float32), jnp.asarray(walsh_table(sub), jnp.float32))
    outer = jnp.einsum("rbm,bc->rcm", inner, mixing, precision=lax.Precision.HIGHEST)
    factor = 1.0 / math.sqrt(units * tp_count)
    turned = (outer * factor).astype(jnp.bfloat16).reshape(share, tp_count, units)
    result = jnp.zeros((rows, units), jnp.bfloat16)
    for distance in range(tp_count):
        block = turned[:, distance]
        if distance:
            block = lax.ppermute(block, "tp", pairs(distance))
        result = lax.dynamic_update_slice_in_dim(result, block, (me ^ distance) * share, 0)
    return result


def shards(hidden, down_weight, channel_scale):
    seq_count = lax.axis_size("seq")
    tp_count = lax.axis_size("tp")
    tokens, units = hidden.shape
    groups = tp_count // seq_count
    owned = tokens // groups
    piece = owned // CHUNKS
    grouped = hidden.reshape(groups, CHUNKS, piece, units)
    outputs = []
    for chunk in range(CHUNKS):
        part = grouped[:, chunk].reshape(groups * piece, units)
        if tp_count == 8:
            rotated = spread_rotate_return(part)
        else:
            spread = lax.all_to_all(part, "tp", split_axis=0, concat_axis=1, tiled=True)
            turned = rotate(spread)
            rotated = lax.all_to_all(turned, "tp", split_axis=1, concat_axis=0, tiled=True)
        partial_terms = gathered_product(rotated, down_weight)
        outputs.append(lax.psum_scatter(partial_terms, "tp", scatter_dimension=0, tiled=True))
    summed = jnp.concatenate(outputs, axis=0)
    return (summed * channel_scale[None, :]).astype(jnp.bfloat16)


def solution(mesh):
    placed = (P("seq", "tp"), P("tp", "seq"), P("seq"))
    return jax.shard_map(
        shards, mesh=mesh, in_specs=placed, out_specs=P("tp", "seq"), check_vma=False
    )
```

```python
import math

import jax
import jax.numpy as jnp
import numpy as np
from jax import lax
from jax.sharding import PartitionSpec as P

PALEY = 28
INNER = 32
CHUNKS = 1


def paley_table():
    residues = set((value * value % 13 for value in range(1, 13)))
    conference = np.zeros((14, 14))
    conference[0, 1:] = 1.0
    conference[1:, 0] = 1.0
    for first in range(13):
        for second in range(13):
            gap = (second - first) % 13
            if gap != 0:
                conference[1 + first, 1 + second] = 1.0 if gap in residues else -1.0
    upper = np.array([[1.0, 1.0], [1.0, -1.0]])
    lower = np.array([[1.0, -1.0], [-1.0, -1.0]])
    return np.kron(conference, upper) + np.kron(np.eye(14), lower)


def walsh_table(order):
    index_rows = np.arange(order)[:, None]
    index_cols = np.arange(order)[None, :]
    signs = np.ones((order, order))
    bit_value = 1
    while bit_value < order:
        both_set = index_rows // bit_value % 2 * (index_cols // bit_value % 2)
        signs = signs * (1 - 2 * both_set)
        bit_value = bit_value * 2
    return signs


def rotate(spread):
    rows, total_units = spread.shape
    walsh = total_units // PALEY
    outer_order = walsh // INNER
    width = INNER * PALEY
    inner_table = jnp.asarray(np.kron(walsh_table(INNER), paley_table()), jnp.bfloat16)
    outer_table = jnp.asarray(walsh_table(outer_order), jnp.float32)
    blocks = spread.reshape(rows, outer_order, width)
    inner = jnp.einsum("rbl,lm->rbm", blocks, inner_table, preferred_element_type=jnp.float32)
    outer = jnp.einsum("rbm,bc->rcm", inner, outer_table, precision=lax.Precision.HIGHEST)
    factor = 1.0 / math.sqrt(total_units)
    return (outer * factor).astype(jnp.bfloat16).reshape(rows, total_units)


def gathered_product(block, down_weight):
    seq_count = lax.axis_size("seq")
    if seq_count != 4:
        gathered = lax.all_gather(block, "seq", axis=0, tiled=True)
        return jnp.dot(gathered, down_weight, preferred_element_type=jnp.float32)
    rows = block.shape[0]
    half = rows // 2
    across_x = lax.ppermute(block, "seq", [(s, s ^ 1) for s in range(4)])
    across_y = lax.ppermute(block, "seq", [(s, s ^ 2) for s in range(4)])
    first = lax.ppermute(across_y[:half], "seq", [(s, s ^ 1) for s in range(4)])
    second = lax.ppermute(across_x[half:], "seq", [(s, s ^ 2) for s in range(4)])
    diagonal = jnp.concatenate([first, second], axis=0)
    me = lax.axis_index("seq")
    columns = down_weight.shape[1]
    result = jnp.zeros((4 * rows, columns), jnp.float32)
    for other, piece in enumerate((block, across_x, across_y, diagonal)):
        product = jnp.dot(piece, down_weight, preferred_element_type=jnp.float32)
        result = lax.dynamic_update_slice_in_dim(result, product, (me ^ other) * rows, 0)
    return result


def spread_rotate_return(part):
    tp_count = lax.axis_size("tp")
    rows, units = part.shape
    share = rows // tp_count
    width = INNER * PALEY
    sub = units // width
    me = lax.axis_index("tp")
    pairs = lambda distance: [(k, k ^ distance) for k in range(tp_count)]
    inner_table = jnp.asarray(np.kron(walsh_table(INNER), paley_table()), jnp.bfloat16)
    landed = []
    for distance in range(tp_count):
        send = lax.dynamic_slice_in_dim(part, (me ^ distance) * share, share, 0)
        if distance:
            send = lax.ppermute(send, "tp", pairs(distance))
        landed.append(
            jnp.einsum(
                "rbl,lm->rbm",
                send.reshape(share, sub, width),
                inner_table,
                preferred_element_type=jnp.float32,
            )
        )
    inner = jnp.stack(landed, axis=1).reshape(share, tp_count * sub, width)
    order = jnp.arange(tp_count, dtype=jnp.int32)
    source = me ^ order
    signs = 1 - 2 * (lax.population_count(source[:, None] & source[None, :]) % 2)
    mixing = jnp.kron(signs.astype(jnp.float32), jnp.asarray(walsh_table(sub), jnp.float32))
    outer = jnp.einsum("rbm,bc->rcm", inner, mixing, precision=lax.Precision.HIGHEST)
    factor = 1.0 / math.sqrt(units * tp_count)
    turned = (outer * factor).astype(jnp.bfloat16).reshape(share, tp_count, units)
    result = jnp.zeros((rows, units), jnp.bfloat16)
    for distance in range(tp_count):
        block = turned[:, distance]
        if distance:
            block = lax.ppermute(block, "tp", pairs(distance))
        result = lax.dynamic_update_slice_in_dim(result, block, (me ^ distance) * share, 0)
    return result


def shards(hidden, down_weight, channel_scale):
    seq_count = lax.axis_size("seq")
    tp_count = lax.axis_size("tp")
    tokens, units = hidden.shape
    groups = tp_count // seq_count
    owned = tokens // groups
    piece = owned // CHUNKS
    grouped = hidden.reshape(groups, CHUNKS, piece, units)
    outputs = []
    for chunk in range(CHUNKS):
        part = grouped[:, chunk].reshape(groups * piece, units)
        if tp_count == 8:
            rotated = spread_rotate_return(part)
        else:
            spread = lax.all_to_all(part, "tp", split_axis=0, concat_axis=1, tiled=True)
            turned = rotate(spread)
            rotated = lax.all_to_all(turned, "tp", split_axis=1, concat_axis=0, tiled=True)
        partial_terms = gathered_product(rotated, down_weight)
        outputs.append(lax.psum_scatter(partial_terms, "tp", scatter_dimension=0, tiled=True))
    summed = jnp.concatenate(outputs, axis=0)
    return (summed * channel_scale[None, :]).astype(jnp.bfloat16)


def solution(mesh):
    placed = (P("seq", "tp"), P("tp", "seq"), P("seq"))
    return jax.shard_map(
        shards, mesh=mesh, in_specs=placed, out_specs=P("tp", "seq"), check_vma=False
    )
```

```python
import math

import jax
import jax.numpy as jnp
import numpy as np
from jax import lax
from jax.sharding import PartitionSpec as P

PALEY = 28
INNER = 32
CHUNKS = 1


def paley_table():
    residues = set((value * value % 13 for value in range(1, 13)))
    conference = np.zeros((14, 14))
    conference[0, 1:] = 1.0
    conference[1:, 0] = 1.0
    for first in range(13):
        for second in range(13):
            gap = (second - first) % 13
            if gap != 0:
                conference[1 + first, 1 + second] = 1.0 if gap in residues else -1.0
    upper = np.array([[1.0, 1.0], [1.0, -1.0]])
    lower = np.array([[1.0, -1.0], [-1.0, -1.0]])
    return np.kron(conference, upper) + np.kron(np.eye(14), lower)


def walsh_table(order):
    index_rows = np.arange(order)[:, None]
    index_cols = np.arange(order)[None, :]
    signs = np.ones((order, order))
    bit_value = 1
    while bit_value < order:
        both_set = index_rows // bit_value % 2 * (index_cols // bit_value % 2)
        signs = signs * (1 - 2 * both_set)
        bit_value = bit_value * 2
    return signs


def rotate(spread):
    rows, total_units = spread.shape
    walsh = total_units // PALEY
    outer_order = walsh // INNER
    width = INNER * PALEY
    inner_table = jnp.asarray(np.kron(walsh_table(INNER), paley_table()), jnp.bfloat16)
    outer_table = jnp.asarray(walsh_table(outer_order), jnp.float32)
    blocks = spread.reshape(rows, outer_order, width)
    inner = jnp.einsum("rbl,lm->rbm", blocks, inner_table, preferred_element_type=jnp.float32)
    outer = jnp.einsum("rbm,bc->rcm", inner, outer_table, precision=lax.Precision.HIGHEST)
    factor = 1.0 / math.sqrt(total_units)
    return (outer * factor).astype(jnp.bfloat16).reshape(rows, total_units)


def gathered_product(block, down_weight):
    seq_count = lax.axis_size("seq")
    if seq_count != 4:
        gathered = lax.all_gather(block, "seq", axis=0, tiled=True)
        return jnp.dot(gathered, down_weight, preferred_element_type=jnp.float32)
    rows = block.shape[0]
    half = rows // 2
    across_x = lax.ppermute(block, "seq", [(s, s ^ 1) for s in range(4)])
    across_y = lax.ppermute(block, "seq", [(s, s ^ 2) for s in range(4)])
    first = lax.ppermute(across_y[:half], "seq", [(s, s ^ 1) for s in range(4)])
    second = lax.ppermute(across_x[half:], "seq", [(s, s ^ 2) for s in range(4)])
    diagonal = jnp.concatenate([first, second], axis=0)
    me = lax.axis_index("seq")
    columns = down_weight.shape[1]
    result = jnp.zeros((4 * rows, columns), jnp.float32)
    for other, piece in enumerate((block, across_x, across_y, diagonal)):
        product = jnp.dot(piece, down_weight, preferred_element_type=jnp.float32)
        result = lax.dynamic_update_slice_in_dim(result, product, (me ^ other) * rows, 0)
    return result


def scatter_sum_tp(partial_terms):
    tp_count = lax.axis_size("tp")
    if tp_count != 8:
        return lax.psum_scatter(partial_terms, "tp", scatter_dimension=0, tiled=True)
    rows, columns = partial_terms.shape
    share = rows // tp_count
    me = lax.axis_index("tp")
    pairs = lambda distance: [(k, k ^ distance) for k in range(tp_count)]
    blocks = partial_terms.reshape(2, 2, 2, share, columns)
    low = me % 2
    keep = lax.dynamic_index_in_dim(blocks, low, 2, keepdims=False)
    send = lax.dynamic_index_in_dim(blocks, 1 - low, 2, keepdims=False)
    summed = keep + lax.ppermute(send, "tp", pairs(1))
    middle = me // 2 % 2
    keep = lax.dynamic_index_in_dim(summed, middle, 1, keepdims=False)
    send = lax.dynamic_index_in_dim(summed, 1 - middle, 1, keepdims=False)
    summed = keep + lax.ppermute(send, "tp", pairs(2))
    high = me // 4 % 2
    keep = lax.dynamic_index_in_dim(summed, high, 0, keepdims=False)
    send = lax.dynamic_index_in_dim(summed, 1 - high, 0, keepdims=False)
    return keep + lax.ppermute(send, "tp", pairs(4))


def shards(hidden, down_weight, channel_scale):
    seq_count = lax.axis_size("seq")
    tp_count = lax.axis_size("tp")
    tokens, units = hidden.shape
    groups = tp_count // seq_count
    owned = tokens // groups
    piece = owned // CHUNKS
    grouped = hidden.reshape(groups, CHUNKS, piece, units)
    outputs = []
    for chunk in range(CHUNKS):
        part = grouped[:, chunk].reshape(groups * piece, units)
        spread = lax.all_to_all(part, "tp", split_axis=0, concat_axis=1, tiled=True)
        turned = rotate(spread)
        rotated = lax.all_to_all(turned, "tp", split_axis=1, concat_axis=0, tiled=True)
        partial_terms = gathered_product(rotated, down_weight)
        outputs.append(scatter_sum_tp(partial_terms))
    summed = jnp.concatenate(outputs, axis=0)
    return (summed * channel_scale[None, :]).astype(jnp.bfloat16)


def solution(mesh):
    placed = (P("seq", "tp"), P("tp", "seq"), P("seq"))
    return jax.shard_map(
        shards, mesh=mesh, in_specs=placed, out_specs=P("tp", "seq"), check_vma=False
    )
```

```python
import math

import jax
import jax.numpy as jnp
import numpy as np
from jax import lax
from jax.sharding import PartitionSpec as P

PALEY = 28
INNER = 32
CHUNKS = 1


def paley_table():
    residues = set((value * value % 13 for value in range(1, 13)))
    conference = np.zeros((14, 14))
    conference[0, 1:] = 1.0
    conference[1:, 0] = 1.0
    for first in range(13):
        for second in range(13):
            gap = (second - first) % 13
            if gap != 0:
                conference[1 + first, 1 + second] = 1.0 if gap in residues else -1.0
    upper = np.array([[1.0, 1.0], [1.0, -1.0]])
    lower = np.array([[1.0, -1.0], [-1.0, -1.0]])
    return np.kron(conference, upper) + np.kron(np.eye(14), lower)


def walsh_table(order):
    index_rows = np.arange(order)[:, None]
    index_cols = np.arange(order)[None, :]
    signs = np.ones((order, order))
    bit_value = 1
    while bit_value < order:
        both_set = index_rows // bit_value % 2 * (index_cols // bit_value % 2)
        signs = signs * (1 - 2 * both_set)
        bit_value = bit_value * 2
    return signs


def rotate(spread):
    rows, total_units = spread.shape
    walsh = total_units // PALEY
    outer_order = walsh // INNER
    width = INNER * PALEY
    inner_table = jnp.asarray(np.kron(walsh_table(INNER), paley_table()), jnp.bfloat16)
    outer_table = jnp.asarray(walsh_table(outer_order), jnp.float32)
    blocks = spread.reshape(rows, outer_order, width)
    inner = jnp.einsum("rbl,lm->rbm", blocks, inner_table, preferred_element_type=jnp.float32)
    outer = jnp.einsum("rbm,bc->rcm", inner, outer_table, precision=lax.Precision.HIGHEST)
    factor = 1.0 / math.sqrt(total_units)
    return (outer * factor).astype(jnp.bfloat16).reshape(rows, total_units)


def gathered_product(block, down_weight):
    seq_count = lax.axis_size("seq")
    if seq_count != 4:
        gathered = lax.all_gather(block, "seq", axis=0, tiled=True)
        return jnp.dot(gathered, down_weight, preferred_element_type=jnp.float32)
    rows = block.shape[0]
    half = rows // 2
    across_x = lax.ppermute(block, "seq", [(s, s ^ 1) for s in range(4)])
    across_y = lax.ppermute(block, "seq", [(s, s ^ 2) for s in range(4)])
    first = lax.ppermute(across_y[:half], "seq", [(s, s ^ 1) for s in range(4)])
    second = lax.ppermute(across_x[half:], "seq", [(s, s ^ 2) for s in range(4)])
    diagonal = jnp.concatenate([first, second], axis=0)
    me = lax.axis_index("seq")
    columns = down_weight.shape[1]
    result = jnp.zeros((4 * rows, columns), jnp.float32)
    for other, piece in enumerate((block, across_x, across_y, diagonal)):
        product = jnp.dot(piece, down_weight, preferred_element_type=jnp.float32)
        result = lax.dynamic_update_slice_in_dim(result, product, (me ^ other) * rows, 0)
    return result


def scatter_sum_tp(partial_terms):
    tp_count = lax.axis_size("tp")
    if tp_count != 8:
        return lax.psum_scatter(partial_terms, "tp", scatter_dimension=0, tiled=True)
    rows, columns = partial_terms.shape
    share = rows // tp_count
    me = lax.axis_index("tp")
    pairs = lambda distance: [(k, k ^ distance) for k in range(tp_count)]
    blocks = partial_terms.reshape(2, 2, 2, share, columns)
    low = me % 2
    keep = lax.dynamic_index_in_dim(blocks, low, 2, keepdims=False)
    send = lax.dynamic_index_in_dim(blocks, 1 - low, 2, keepdims=False)
    summed = keep + lax.ppermute(send, "tp", pairs(1))
    middle = me // 2 % 2
    keep = lax.dynamic_index_in_dim(summed, middle, 1, keepdims=False)
    send = lax.dynamic_index_in_dim(summed, 1 - middle, 1, keepdims=False)
    summed = keep + lax.ppermute(send, "tp", pairs(2))
    high = me // 4 % 2
    keep = lax.dynamic_index_in_dim(summed, high, 0, keepdims=False)
    send = lax.dynamic_index_in_dim(summed, 1 - high, 0, keepdims=False)
    return keep + lax.ppermute(send, "tp", pairs(4))


def product_and_reduce(block, down_weight):
    rows = block.shape[0]
    half = rows // 2
    seq_pairs = lambda distance: [(s, s ^ distance) for s in range(4)]
    tp_pairs = lambda distance: [(k, k ^ distance) for k in range(8)]
    here = lax.axis_index("seq")
    me = lax.axis_index("tp")
    low, middle, high = me % 2, me // 2 % 2, me // 4 % 2
    across_x = lax.ppermute(block, "seq", seq_pairs(1))
    across_y = lax.ppermute(block, "seq", seq_pairs(2))
    first = lax.ppermute(across_y[:half], "seq", seq_pairs(1))
    second = lax.ppermute(across_x[half:], "seq", seq_pairs(2))
    diagonal = jnp.concatenate([first, second], axis=0)

    def halve_pair(pieces):
        products = jnp.stack(
            [jnp.dot(piece, down_weight, preferred_element_type=jnp.float32) for piece in pieces]
        )
        split = products.reshape(2, 2, half, products.shape[-1])
        keep = lax.dynamic_index_in_dim(split, low, 1, keepdims=False)
        send = lax.dynamic_index_in_dim(split, 1 - low, 1, keepdims=False)
        summed = keep + lax.ppermute(send, "tp", tp_pairs(1))
        chosen = here % 2 ^ middle
        keep = lax.dynamic_index_in_dim(summed, chosen, 0, keepdims=False)
        send = lax.dynamic_index_in_dim(summed, 1 - chosen, 0, keepdims=False)
        return keep + lax.ppermute(send, "tp", tp_pairs(2))

    near = halve_pair((block, across_x))
    far = halve_pair((across_y, diagonal))
    both = jnp.stack([near, far])
    chosen = here // 2 % 2 ^ high
    keep = lax.dynamic_index_in_dim(both, chosen, 0, keepdims=False)
    send = lax.dynamic_index_in_dim(both, 1 - chosen, 0, keepdims=False)
    return keep + lax.ppermute(send, "tp", tp_pairs(4))


def shards(hidden, down_weight, channel_scale):
    seq_count = lax.axis_size("seq")
    tp_count = lax.axis_size("tp")
    tokens, units = hidden.shape
    groups = tp_count // seq_count
    owned = tokens // groups
    piece = owned // CHUNKS
    grouped = hidden.reshape(groups, CHUNKS, piece, units)
    outputs = []
    for chunk in range(CHUNKS):
        part = grouped[:, chunk].reshape(groups * piece, units)
        spread = lax.all_to_all(part, "tp", split_axis=0, concat_axis=1, tiled=True)
        turned = rotate(spread)
        rotated = lax.all_to_all(turned, "tp", split_axis=1, concat_axis=0, tiled=True)
        if seq_count == 4 and tp_count == 8:
            outputs.append(product_and_reduce(rotated, down_weight))
        else:
            partial_terms = gathered_product(rotated, down_weight)
            outputs.append(scatter_sum_tp(partial_terms))
    summed = jnp.concatenate(outputs, axis=0)
    return (summed * channel_scale[None, :]).astype(jnp.bfloat16)


def solution(mesh):
    placed = (P("seq", "tp"), P("tp", "seq"), P("seq"))
    return jax.shard_map(
        shards, mesh=mesh, in_specs=placed, out_specs=P("tp", "seq"), check_vma=False
    )
```

```python
import math

import jax
import jax.numpy as jnp
import numpy as np
from jax import lax
from jax.sharding import PartitionSpec as P

PALEY = 28
INNER = 32
CHUNKS = 2


def paley_table():
    residues = set((value * value % 13 for value in range(1, 13)))
    conference = np.zeros((14, 14))
    conference[0, 1:] = 1.0
    conference[1:, 0] = 1.0
    for first in range(13):
        for second in range(13):
            gap = (second - first) % 13
            if gap != 0:
                conference[1 + first, 1 + second] = 1.0 if gap in residues else -1.0
    upper = np.array([[1.0, 1.0], [1.0, -1.0]])
    lower = np.array([[1.0, -1.0], [-1.0, -1.0]])
    return np.kron(conference, upper) + np.kron(np.eye(14), lower)


def walsh_table(order):
    index_rows = np.arange(order)[:, None]
    index_cols = np.arange(order)[None, :]
    signs = np.ones((order, order))
    bit_value = 1
    while bit_value < order:
        both_set = index_rows // bit_value % 2 * (index_cols // bit_value % 2)
        signs = signs * (1 - 2 * both_set)
        bit_value = bit_value * 2
    return signs


def rotate(spread):
    rows, total_units = spread.shape
    walsh = total_units // PALEY
    outer_order = walsh // INNER
    width = INNER * PALEY
    inner_table = jnp.asarray(np.kron(walsh_table(INNER), paley_table()), jnp.bfloat16)
    outer_table = jnp.asarray(walsh_table(outer_order), jnp.float32)
    blocks = spread.reshape(rows, outer_order, width)
    inner = jnp.einsum("rbl,lm->rbm", blocks, inner_table, preferred_element_type=jnp.float32)
    outer = jnp.einsum("rbm,bc->rcm", inner, outer_table, precision=lax.Precision.HIGHEST)
    factor = 1.0 / math.sqrt(total_units)
    return (outer * factor).astype(jnp.bfloat16).reshape(rows, total_units)


def gathered_product(block, down_weight):
    seq_count = lax.axis_size("seq")
    if seq_count != 4:
        gathered = lax.all_gather(block, "seq", axis=0, tiled=True)
        return jnp.dot(gathered, down_weight, preferred_element_type=jnp.float32)
    rows = block.shape[0]
    half = rows // 2
    across_x = lax.ppermute(block, "seq", [(s, s ^ 1) for s in range(4)])
    across_y = lax.ppermute(block, "seq", [(s, s ^ 2) for s in range(4)])
    first = lax.ppermute(across_y[:half], "seq", [(s, s ^ 1) for s in range(4)])
    second = lax.ppermute(across_x[half:], "seq", [(s, s ^ 2) for s in range(4)])
    diagonal = jnp.concatenate([first, second], axis=0)
    me = lax.axis_index("seq")
    columns = down_weight.shape[1]
    result = jnp.zeros((4 * rows, columns), jnp.float32)
    for other, piece in enumerate((block, across_x, across_y, diagonal)):
        product = jnp.dot(piece, down_weight, preferred_element_type=jnp.float32)
        result = lax.dynamic_update_slice_in_dim(result, product, (me ^ other) * rows, 0)
    return result


def scatter_sum_tp(partial_terms):
    tp_count = lax.axis_size("tp")
    if tp_count != 8:
        return lax.psum_scatter(partial_terms, "tp", scatter_dimension=0, tiled=True)
    rows, columns = partial_terms.shape
    share = rows // tp_count
    me = lax.axis_index("tp")
    pairs = lambda distance: [(k, k ^ distance) for k in range(tp_count)]
    blocks = partial_terms.reshape(2, 2, 2, share, columns)
    low = me % 2
    keep = lax.dynamic_index_in_dim(blocks, low, 2, keepdims=False)
    send = lax.dynamic_index_in_dim(blocks, 1 - low, 2, keepdims=False)
    summed = keep + lax.ppermute(send, "tp", pairs(1))
    middle = me // 2 % 2
    keep = lax.dynamic_index_in_dim(summed, middle, 1, keepdims=False)
    send = lax.dynamic_index_in_dim(summed, 1 - middle, 1, keepdims=False)
    summed = keep + lax.ppermute(send, "tp", pairs(2))
    high = me // 4 % 2
    keep = lax.dynamic_index_in_dim(summed, high, 0, keepdims=False)
    send = lax.dynamic_index_in_dim(summed, 1 - high, 0, keepdims=False)
    return keep + lax.ppermute(send, "tp", pairs(4))


def product_and_reduce(block, down_weight):
    rows = block.shape[0]
    half = rows // 2
    seq_pairs = lambda distance: [(s, s ^ distance) for s in range(4)]
    tp_pairs = lambda distance: [(k, k ^ distance) for k in range(8)]
    here = lax.axis_index("seq")
    me = lax.axis_index("tp")
    low, middle, high = me % 2, me // 2 % 2, me // 4 % 2
    across_x = lax.ppermute(block, "seq", seq_pairs(1))
    across_y = lax.ppermute(block, "seq", seq_pairs(2))
    first = lax.ppermute(across_y[:half], "seq", seq_pairs(1))
    second = lax.ppermute(across_x[half:], "seq", seq_pairs(2))
    diagonal = jnp.concatenate([first, second], axis=0)

    def halve_pair(pieces):
        products = jnp.stack(
            [jnp.dot(piece, down_weight, preferred_element_type=jnp.float32) for piece in pieces]
        )
        split = products.reshape(2, 2, half, products.shape[-1])
        keep = lax.dynamic_index_in_dim(split, low, 1, keepdims=False)
        send = lax.dynamic_index_in_dim(split, 1 - low, 1, keepdims=False)
        summed = keep + lax.ppermute(send, "tp", tp_pairs(1))
        chosen = here % 2 ^ middle
        keep = lax.dynamic_index_in_dim(summed, chosen, 0, keepdims=False)
        send = lax.dynamic_index_in_dim(summed, 1 - chosen, 0, keepdims=False)
        return keep + lax.ppermute(send, "tp", tp_pairs(2))

    near = halve_pair((block, across_x))
    far = halve_pair((across_y, diagonal))
    both = jnp.stack([near, far])
    chosen = here // 2 % 2 ^ high
    keep = lax.dynamic_index_in_dim(both, chosen, 0, keepdims=False)
    send = lax.dynamic_index_in_dim(both, 1 - chosen, 0, keepdims=False)
    return keep + lax.ppermute(send, "tp", tp_pairs(4))


def shards(hidden, down_weight, channel_scale):
    seq_count = lax.axis_size("seq")
    tp_count = lax.axis_size("tp")
    tokens, units = hidden.shape
    groups = tp_count // seq_count
    owned = tokens // groups
    piece = owned // CHUNKS
    grouped = hidden.reshape(groups, CHUNKS, piece, units)
    fast_path = seq_count == 4 and tp_count == 8
    outputs = []
    pending = None
    for chunk in range(CHUNKS):
        part = grouped[:, chunk].reshape(groups * piece, units)
        if pending is not None:
            pending, part = lax.optimization_barrier((pending, part))
            outputs.append(product_and_reduce(pending, down_weight))
        spread = lax.all_to_all(part, "tp", split_axis=0, concat_axis=1, tiled=True)
        turned = rotate(spread)
        rotated = lax.all_to_all(turned, "tp", split_axis=1, concat_axis=0, tiled=True)
        if fast_path:
            pending = rotated
        else:
            partial_terms = gathered_product(rotated, down_weight)
            outputs.append(scatter_sum_tp(partial_terms))
    if pending is not None:
        outputs.append(product_and_reduce(pending, down_weight))
    summed = jnp.concatenate(outputs, axis=0)
    return (summed * channel_scale[None, :]).astype(jnp.bfloat16)


def solution(mesh):
    placed = (P("seq", "tp"), P("tp", "seq"), P("seq"))
    return jax.shard_map(
        shards, mesh=mesh, in_specs=placed, out_specs=P("tp", "seq"), check_vma=False
    )
```

```python
import math

import jax
import jax.numpy as jnp
import numpy as np
from jax import lax
from jax.sharding import PartitionSpec as P

PALEY = 28
INNER = 32
CHUNKS = 1


def paley_table():
    residues = set((value * value % 13 for value in range(1, 13)))
    conference = np.zeros((14, 14))
    conference[0, 1:] = 1.0
    conference[1:, 0] = 1.0
    for first in range(13):
        for second in range(13):
            gap = (second - first) % 13
            if gap != 0:
                conference[1 + first, 1 + second] = 1.0 if gap in residues else -1.0
    upper = np.array([[1.0, 1.0], [1.0, -1.0]])
    lower = np.array([[1.0, -1.0], [-1.0, -1.0]])
    return np.kron(conference, upper) + np.kron(np.eye(14), lower)


def walsh_table(order):
    index_rows = np.arange(order)[:, None]
    index_cols = np.arange(order)[None, :]
    signs = np.ones((order, order))
    bit_value = 1
    while bit_value < order:
        both_set = index_rows // bit_value % 2 * (index_cols // bit_value % 2)
        signs = signs * (1 - 2 * both_set)
        bit_value = bit_value * 2
    return signs


def rotate(spread):
    rows, total_units = spread.shape
    walsh = total_units // PALEY
    outer_order = walsh // INNER
    width = INNER * PALEY
    inner_table = jnp.asarray(np.kron(walsh_table(INNER), paley_table()), jnp.bfloat16)
    outer_table = jnp.asarray(walsh_table(outer_order), jnp.float32)
    blocks = spread.reshape(rows, outer_order, width)
    inner = jnp.einsum("rbl,lm->rbm", blocks, inner_table, preferred_element_type=jnp.float32)
    outer = jnp.einsum("rbm,bc->rcm", inner, outer_table, precision=lax.Precision.HIGHEST)
    factor = 1.0 / math.sqrt(total_units)
    return (outer * factor).astype(jnp.bfloat16).reshape(rows, total_units)


def gathered_product(block, down_weight):
    seq_count = lax.axis_size("seq")
    if seq_count != 4:
        gathered = lax.all_gather(block, "seq", axis=0, tiled=True)
        return jnp.dot(gathered, down_weight, preferred_element_type=jnp.float32)
    rows = block.shape[0]
    half = rows // 2
    across_x = lax.ppermute(block, "seq", [(s, s ^ 1) for s in range(4)])
    across_y = lax.ppermute(block, "seq", [(s, s ^ 2) for s in range(4)])
    first = lax.ppermute(across_y[:half], "seq", [(s, s ^ 1) for s in range(4)])
    second = lax.ppermute(across_x[half:], "seq", [(s, s ^ 2) for s in range(4)])
    diagonal = jnp.concatenate([first, second], axis=0)
    me = lax.axis_index("seq")
    columns = down_weight.shape[1]
    result = jnp.zeros((4 * rows, columns), jnp.float32)
    for other, piece in enumerate((block, across_x, across_y, diagonal)):
        product = jnp.dot(piece, down_weight, preferred_element_type=jnp.float32)
        result = lax.dynamic_update_slice_in_dim(result, product, (me ^ other) * rows, 0)
    return result


def scatter_sum_tp(partial_terms):
    tp_count = lax.axis_size("tp")
    if tp_count != 8:
        return lax.psum_scatter(partial_terms, "tp", scatter_dimension=0, tiled=True)
    rows, columns = partial_terms.shape
    share = rows // tp_count
    me = lax.axis_index("tp")
    pairs = lambda distance: [(k, k ^ distance) for k in range(tp_count)]
    blocks = partial_terms.reshape(2, 2, 2, share, columns)
    low = me % 2
    keep = lax.dynamic_index_in_dim(blocks, low, 2, keepdims=False)
    send = lax.dynamic_index_in_dim(blocks, 1 - low, 2, keepdims=False)
    summed = keep + lax.ppermute(send, "tp", pairs(1))
    middle = me // 2 % 2
    keep = lax.dynamic_index_in_dim(summed, middle, 1, keepdims=False)
    send = lax.dynamic_index_in_dim(summed, 1 - middle, 1, keepdims=False)
    summed = keep + lax.ppermute(send, "tp", pairs(2))
    high = me // 4 % 2
    keep = lax.dynamic_index_in_dim(summed, high, 0, keepdims=False)
    send = lax.dynamic_index_in_dim(summed, 1 - high, 0, keepdims=False)
    return keep + lax.ppermute(send, "tp", pairs(4))


def product_and_reduce(block, down_weight, channel_scale):
    rows = block.shape[0]
    half = rows // 2
    seq_pairs = lambda distance: [(s, s ^ distance) for s in range(4)]
    tp_pairs = lambda distance: [(k, k ^ distance) for k in range(8)]
    here = lax.axis_index("seq")
    me = lax.axis_index("tp")
    low, middle, high = me % 2, me // 2 % 2, me // 4 % 2
    across_x = lax.ppermute(block, "seq", seq_pairs(1))
    across_y = lax.ppermute(block, "seq", seq_pairs(2))
    first = lax.ppermute(across_y[:half], "seq", seq_pairs(1))
    second = lax.ppermute(across_x[half:], "seq", seq_pairs(2))
    diagonal = jnp.concatenate([first, second], axis=0)

    def halve_pair(pieces):
        products = jnp.stack(
            [jnp.dot(piece, down_weight, preferred_element_type=jnp.float32) for piece in pieces]
        )
        split = products.reshape(2, 2, half, products.shape[-1])
        keep = lax.dynamic_index_in_dim(split, low, 1, keepdims=False)
        send = lax.dynamic_index_in_dim(split, 1 - low, 1, keepdims=False)
        summed = keep + lax.ppermute(send, "tp", tp_pairs(1))
        chosen = here % 2 ^ middle
        keep = lax.dynamic_index_in_dim(summed, chosen, 0, keepdims=False)
        send = lax.dynamic_index_in_dim(summed, 1 - chosen, 0, keepdims=False)
        return keep + lax.ppermute(send, "tp", tp_pairs(2))

    near = halve_pair((block, across_x))
    far = halve_pair((across_y, diagonal))
    columns = near.shape[-1]
    split = columns // 2
    owns_near = here // 2 % 2 == high
    both = ("seq", "tp")
    side_pairs = lambda owner: [
        (s * 8 + k, s * 8 + (k ^ 4))
        for s in range(4)
        for k in range(8)
        if (k // 4 % 2 == s // 2 % 2) == owner
    ]
    from_far_side = side_pairs(False)
    from_near_side = side_pairs(True)
    near_in = lax.ppermute(near, both, from_far_side)
    far_first_in = lax.ppermute(far[:, :split], both, from_near_side)
    far_second_in = lax.ppermute(far[:, split:], both, from_far_side)
    scale_first, scale_second = channel_scale[:split], channel_scale[split:]
    near_sum = near + near_in
    finished = ((far[:, split:] + far_second_in) * scale_second[None, :]).astype(jnp.bfloat16)
    finished_in = lax.ppermute(finished, both, from_near_side)
    first = jnp.where(owns_near, near_sum[:, :split], far[:, :split] + far_first_in)
    second_near = (near_sum[:, split:] * scale_second[None, :]).astype(jnp.bfloat16)
    second = jnp.where(owns_near, second_near, finished_in)
    first = (first * scale_first[None, :]).astype(jnp.bfloat16)
    return jnp.concatenate([first, second], axis=1)


def shards(hidden, down_weight, channel_scale):
    seq_count = lax.axis_size("seq")
    tp_count = lax.axis_size("tp")
    tokens, units = hidden.shape
    groups = tp_count // seq_count
    owned = tokens // groups
    piece = owned // CHUNKS
    grouped = hidden.reshape(groups, CHUNKS, piece, units)
    outputs = []
    for chunk in range(CHUNKS):
        part = grouped[:, chunk].reshape(groups * piece, units)
        spread = lax.all_to_all(part, "tp", split_axis=0, concat_axis=1, tiled=True)
        turned = rotate(spread)
        rotated = lax.all_to_all(turned, "tp", split_axis=1, concat_axis=0, tiled=True)
        if seq_count == 4 and tp_count == 8:
            outputs.append(product_and_reduce(rotated, down_weight, channel_scale))
        else:
            partial_terms = gathered_product(rotated, down_weight)
            summed = scatter_sum_tp(partial_terms)
            outputs.append((summed * channel_scale[None, :]).astype(jnp.bfloat16))
    return jnp.concatenate(outputs, axis=0)


def solution(mesh):
    placed = (P("seq", "tp"), P("tp", "seq"), P("seq"))
    return jax.shard_map(
        shards, mesh=mesh, in_specs=placed, out_specs=P("tp", "seq"), check_vma=False
    )
```

```python
import math

import jax
import jax.numpy as jnp
import numpy as np
from jax import lax
from jax.sharding import PartitionSpec as P

PALEY = 28
INNER = 32
CHUNKS = 1


def paley_table():
    residues = set((value * value % 13 for value in range(1, 13)))
    conference = np.zeros((14, 14))
    conference[0, 1:] = 1.0
    conference[1:, 0] = 1.0
    for first in range(13):
        for second in range(13):
            gap = (second - first) % 13
            if gap != 0:
                conference[1 + first, 1 + second] = 1.0 if gap in residues else -1.0
    upper = np.array([[1.0, 1.0], [1.0, -1.0]])
    lower = np.array([[1.0, -1.0], [-1.0, -1.0]])
    return np.kron(conference, upper) + np.kron(np.eye(14), lower)


def walsh_table(order):
    index_rows = np.arange(order)[:, None]
    index_cols = np.arange(order)[None, :]
    signs = np.ones((order, order))
    bit_value = 1
    while bit_value < order:
        both_set = index_rows // bit_value % 2 * (index_cols // bit_value % 2)
        signs = signs * (1 - 2 * both_set)
        bit_value = bit_value * 2
    return signs


def rotate(spread):
    rows, total_units = spread.shape
    walsh = total_units // PALEY
    outer_order = walsh // INNER
    width = INNER * PALEY
    inner_table = jnp.asarray(np.kron(walsh_table(INNER), paley_table()), jnp.bfloat16)
    outer_table = jnp.asarray(walsh_table(outer_order), jnp.float32)
    blocks = spread.reshape(rows, outer_order, width)
    inner = jnp.einsum("rbl,lm->rbm", blocks, inner_table, preferred_element_type=jnp.float32)
    outer = jnp.einsum("rbm,bc->rcm", inner, outer_table, precision=lax.Precision.HIGHEST)
    factor = 1.0 / math.sqrt(total_units)
    return (outer * factor).astype(jnp.bfloat16).reshape(rows, total_units)


def gathered_product(block, down_weight):
    seq_count = lax.axis_size("seq")
    if seq_count != 4:
        gathered = lax.all_gather(block, "seq", axis=0, tiled=True)
        return jnp.dot(gathered, down_weight, preferred_element_type=jnp.float32)
    rows = block.shape[0]
    half = rows // 2
    across_x = lax.ppermute(block, "seq", [(s, s ^ 1) for s in range(4)])
    across_y = lax.ppermute(block, "seq", [(s, s ^ 2) for s in range(4)])
    first = lax.ppermute(across_y[:half], "seq", [(s, s ^ 1) for s in range(4)])
    second = lax.ppermute(across_x[half:], "seq", [(s, s ^ 2) for s in range(4)])
    diagonal = jnp.concatenate([first, second], axis=0)
    me = lax.axis_index("seq")
    columns = down_weight.shape[1]
    result = jnp.zeros((4 * rows, columns), jnp.float32)
    for other, piece in enumerate((block, across_x, across_y, diagonal)):
        product = jnp.dot(piece, down_weight, preferred_element_type=jnp.float32)
        result = lax.dynamic_update_slice_in_dim(result, product, (me ^ other) * rows, 0)
    return result


def scatter_sum_tp(partial_terms):
    tp_count = lax.axis_size("tp")
    if tp_count != 8:
        return lax.psum_scatter(partial_terms, "tp", scatter_dimension=0, tiled=True)
    rows, columns = partial_terms.shape
    share = rows // tp_count
    me = lax.axis_index("tp")
    pairs = lambda distance: [(k, k ^ distance) for k in range(tp_count)]
    blocks = partial_terms.reshape(2, 2, 2, share, columns)
    low = me % 2
    keep = lax.dynamic_index_in_dim(blocks, low, 2, keepdims=False)
    send = lax.dynamic_index_in_dim(blocks, 1 - low, 2, keepdims=False)
    summed = keep + lax.ppermute(send, "tp", pairs(1))
    middle = me // 2 % 2
    keep = lax.dynamic_index_in_dim(summed, middle, 1, keepdims=False)
    send = lax.dynamic_index_in_dim(summed, 1 - middle, 1, keepdims=False)
    summed = keep + lax.ppermute(send, "tp", pairs(2))
    high = me // 4 % 2
    keep = lax.dynamic_index_in_dim(summed, high, 0, keepdims=False)
    send = lax.dynamic_index_in_dim(summed, 1 - high, 0, keepdims=False)
    return keep + lax.ppermute(send, "tp", pairs(4))


def spread_rotate_return(part):
    tp_count = lax.axis_size("tp")
    rows, units = part.shape
    share = rows // tp_count
    width = INNER * PALEY
    sub = units // width
    me = lax.axis_index("tp")
    pairs = lambda distance: [(k, k ^ distance) for k in range(tp_count)]
    inner_table = jnp.asarray(np.kron(walsh_table(INNER), paley_table()), jnp.bfloat16)
    landed = []
    for distance in range(tp_count):
        send = lax.dynamic_slice_in_dim(part, (me ^ distance) * share, share, 0)
        if distance:
            send = lax.ppermute(send, "tp", pairs(distance))
        landed.append(
            jnp.einsum(
                "rbl,lm->rbm",
                send.reshape(share, sub, width),
                inner_table,
                preferred_element_type=jnp.float32,
            )
        )
    inner = jnp.stack(landed, axis=1).reshape(share, tp_count * sub, width)
    order = jnp.arange(tp_count, dtype=jnp.int32)
    source = me ^ order
    signs = 1 - 2 * (lax.population_count(source[:, None] & source[None, :]) % 2)
    mixing = jnp.kron(signs.astype(jnp.float32), jnp.asarray(walsh_table(sub), jnp.float32))
    outer = jnp.einsum("rbm,bc->rcm", inner, mixing, precision=lax.Precision.HIGHEST)
    factor = 1.0 / math.sqrt(units * tp_count)
    turned = (outer * factor).astype(jnp.bfloat16).reshape(share, tp_count, units)
    result = jnp.zeros((rows, units), jnp.bfloat16)
    for distance in range(tp_count):
        block = turned[:, distance]
        if distance:
            block = lax.ppermute(block, "tp", pairs(distance))
        result = lax.dynamic_update_slice_in_dim(result, block, (me ^ distance) * share, 0)
    return result


def product_and_reduce(block, down_weight):
    rows = block.shape[0]
    half = rows // 2
    seq_pairs = lambda distance: [(s, s ^ distance) for s in range(4)]
    tp_pairs = lambda distance: [(k, k ^ distance) for k in range(8)]
    here = lax.axis_index("seq")
    me = lax.axis_index("tp")
    low, middle, high = me % 2, me // 2 % 2, me // 4 % 2
    across_x = lax.ppermute(block, "seq", seq_pairs(1))
    across_y = lax.ppermute(block, "seq", seq_pairs(2))
    first = lax.ppermute(across_y[:half], "seq", seq_pairs(1))
    second = lax.ppermute(across_x[half:], "seq", seq_pairs(2))
    diagonal = jnp.concatenate([first, second], axis=0)

    def halve_pair(pieces):
        products = jnp.stack(
            [jnp.dot(piece, down_weight, preferred_element_type=jnp.float32) for piece in pieces]
        )
        split = products.reshape(2, 2, half, products.shape[-1])
        keep = lax.dynamic_index_in_dim(split, low, 1, keepdims=False)
        send = lax.dynamic_index_in_dim(split, 1 - low, 1, keepdims=False)
        summed = keep + lax.ppermute(send, "tp", tp_pairs(1))
        chosen = here % 2 ^ middle
        keep = lax.dynamic_index_in_dim(summed, chosen, 0, keepdims=False)
        send = lax.dynamic_index_in_dim(summed, 1 - chosen, 0, keepdims=False)
        return keep + lax.ppermute(send, "tp", tp_pairs(2))

    near = halve_pair((block, across_x))
    far = halve_pair((across_y, diagonal))
    both = jnp.stack([near, far])
    chosen = here // 2 % 2 ^ high
    keep = lax.dynamic_index_in_dim(both, chosen, 0, keepdims=False)
    send = lax.dynamic_index_in_dim(both, 1 - chosen, 0, keepdims=False)
    return keep + lax.ppermute(send, "tp", tp_pairs(4))


def shards(hidden, down_weight, channel_scale):
    seq_count = lax.axis_size("seq")
    tp_count = lax.axis_size("tp")
    tokens, units = hidden.shape
    groups = tp_count // seq_count
    owned = tokens // groups
    piece = owned // CHUNKS
    grouped = hidden.reshape(groups, CHUNKS, piece, units)
    outputs = []
    for chunk in range(CHUNKS):
        part = grouped[:, chunk].reshape(groups * piece, units)
        if tp_count == 8:
            rotated = spread_rotate_return(part)
        else:
            spread = lax.all_to_all(part, "tp", split_axis=0, concat_axis=1, tiled=True)
            turned = rotate(spread)
            rotated = lax.all_to_all(turned, "tp", split_axis=1, concat_axis=0, tiled=True)
        if seq_count == 4 and tp_count == 8:
            outputs.append(product_and_reduce(rotated, down_weight))
        else:
            partial_terms = gathered_product(rotated, down_weight)
            outputs.append(scatter_sum_tp(partial_terms))
    summed = jnp.concatenate(outputs, axis=0)
    return (summed * channel_scale[None, :]).astype(jnp.bfloat16)


def solution(mesh):
    placed = (P("seq", "tp"), P("tp", "seq"), P("seq"))
    return jax.shard_map(
        shards, mesh=mesh, in_specs=placed, out_specs=P("tp", "seq"), check_vma=False
    )
```

```python
import math

import jax
import jax.numpy as jnp
import numpy as np
from jax import lax
from jax.sharding import PartitionSpec as P

PALEY = 28
INNER = 32
CHUNKS = 1


def paley_table():
    residues = set((value * value % 13 for value in range(1, 13)))
    conference = np.zeros((14, 14))
    conference[0, 1:] = 1.0
    conference[1:, 0] = 1.0
    for first in range(13):
        for second in range(13):
            gap = (second - first) % 13
            if gap != 0:
                conference[1 + first, 1 + second] = 1.0 if gap in residues else -1.0
    upper = np.array([[1.0, 1.0], [1.0, -1.0]])
    lower = np.array([[1.0, -1.0], [-1.0, -1.0]])
    return np.kron(conference, upper) + np.kron(np.eye(14), lower)


def walsh_table(order):
    index_rows = np.arange(order)[:, None]
    index_cols = np.arange(order)[None, :]
    signs = np.ones((order, order))
    bit_value = 1
    while bit_value < order:
        both_set = index_rows // bit_value % 2 * (index_cols // bit_value % 2)
        signs = signs * (1 - 2 * both_set)
        bit_value = bit_value * 2
    return signs


def rotate(spread):
    rows, total_units = spread.shape
    walsh = total_units // PALEY
    outer_order = walsh // INNER
    width = INNER * PALEY
    inner_table = jnp.asarray(np.kron(walsh_table(INNER), paley_table()), jnp.bfloat16)
    outer_table = jnp.asarray(walsh_table(outer_order), jnp.float32)
    blocks = spread.reshape(rows, outer_order, width)
    inner = jnp.einsum("rbl,lm->rbm", blocks, inner_table, preferred_element_type=jnp.float32)
    outer = jnp.einsum("rbm,bc->rcm", inner, outer_table, precision=lax.Precision.HIGHEST)
    factor = 1.0 / math.sqrt(total_units)
    return (outer * factor).astype(jnp.bfloat16).reshape(rows, total_units)


def gathered_product(block, down_weight):
    seq_count = lax.axis_size("seq")
    if seq_count != 4:
        gathered = lax.all_gather(block, "seq", axis=0, tiled=True)
        return jnp.dot(gathered, down_weight, preferred_element_type=jnp.float32)
    rows = block.shape[0]
    half = rows // 2
    across_x = lax.ppermute(block, "seq", [(s, s ^ 1) for s in range(4)])
    across_y = lax.ppermute(block, "seq", [(s, s ^ 2) for s in range(4)])
    first = lax.ppermute(across_y[:half], "seq", [(s, s ^ 1) for s in range(4)])
    second = lax.ppermute(across_x[half:], "seq", [(s, s ^ 2) for s in range(4)])
    diagonal = jnp.concatenate([first, second], axis=0)
    me = lax.axis_index("seq")
    columns = down_weight.shape[1]
    result = jnp.zeros((4 * rows, columns), jnp.float32)
    for other, piece in enumerate((block, across_x, across_y, diagonal)):
        product = jnp.dot(piece, down_weight, preferred_element_type=jnp.float32)
        result = lax.dynamic_update_slice_in_dim(result, product, (me ^ other) * rows, 0)
    return result


def scatter_sum_tp(partial_terms):
    tp_count = lax.axis_size("tp")
    if tp_count != 8:
        return lax.psum_scatter(partial_terms, "tp", scatter_dimension=0, tiled=True)
    rows, columns = partial_terms.shape
    share = rows // tp_count
    me = lax.axis_index("tp")
    pairs = lambda distance: [(k, k ^ distance) for k in range(tp_count)]
    blocks = partial_terms.reshape(2, 2, 2, share, columns)
    low = me % 2
    keep = lax.dynamic_index_in_dim(blocks, low, 2, keepdims=False)
    send = lax.dynamic_index_in_dim(blocks, 1 - low, 2, keepdims=False)
    summed = keep + lax.ppermute(send, "tp", pairs(1))
    middle = me // 2 % 2
    keep = lax.dynamic_index_in_dim(summed, middle, 1, keepdims=False)
    send = lax.dynamic_index_in_dim(summed, 1 - middle, 1, keepdims=False)
    summed = keep + lax.ppermute(send, "tp", pairs(2))
    high = me // 4 % 2
    keep = lax.dynamic_index_in_dim(summed, high, 0, keepdims=False)
    send = lax.dynamic_index_in_dim(summed, 1 - high, 0, keepdims=False)
    return keep + lax.ppermute(send, "tp", pairs(4))


def spread_rotate_return(part):
    tp_count = lax.axis_size("tp")
    rows, units = part.shape
    share = rows // tp_count
    width = INNER * PALEY
    sub = units // width
    me = lax.axis_index("tp")
    pairs = lambda distance: [(k, k ^ distance) for k in range(tp_count)]
    inner_table = jnp.asarray(np.kron(walsh_table(INNER), paley_table()), jnp.bfloat16)
    landed = []
    for distance in range(tp_count):
        send = lax.dynamic_slice_in_dim(part, (me ^ distance) * share, share, 0)
        if distance:
            send = lax.ppermute(send, "tp", pairs(distance))
        landed.append(
            jnp.einsum(
                "rbl,lm->rbm",
                send.reshape(share, sub, width),
                inner_table,
                preferred_element_type=jnp.float32,
            )
        )
    inner = jnp.stack(landed, axis=1).reshape(share, tp_count * sub, width)
    order = jnp.arange(tp_count, dtype=jnp.int32)
    source = me ^ order
    signs = 1 - 2 * (lax.population_count(source[:, None] & source[None, :]) % 2)
    mixing = jnp.kron(signs.astype(jnp.float32), jnp.asarray(walsh_table(sub), jnp.float32))
    outer = jnp.einsum("rbm,bc->rcm", inner, mixing, precision=lax.Precision.HIGHEST)
    factor = 1.0 / math.sqrt(units * tp_count)
    turned = (outer * factor).astype(jnp.bfloat16).reshape(share, tp_count, units)
    result = jnp.zeros((rows, units), jnp.bfloat16)
    for distance in range(tp_count):
        block = turned[:, distance]
        if distance:
            block = lax.ppermute(block, "tp", pairs(distance))
        result = lax.dynamic_update_slice_in_dim(result, block, (me ^ distance) * share, 0)
    return result


def product_and_reduce(block, down_weight):
    rows = block.shape[0]
    half = rows // 2
    seq_pairs = lambda distance: [(s, s ^ distance) for s in range(4)]
    tp_pairs = lambda distance: [(k, k ^ distance) for k in range(8)]
    here = lax.axis_index("seq")
    me = lax.axis_index("tp")
    low, middle, high = me % 2, me // 2 % 2, me // 4 % 2
    across_x = lax.ppermute(block, "seq", seq_pairs(1))
    across_y = lax.ppermute(block, "seq", seq_pairs(2))
    first = lax.ppermute(across_y[:half], "seq", seq_pairs(1))
    second = lax.ppermute(across_x[half:], "seq", seq_pairs(2))
    diagonal = jnp.concatenate([first, second], axis=0)

    def first_halving(pieces):
        products = jnp.stack(
            [jnp.dot(piece, down_weight, preferred_element_type=jnp.float32) for piece in pieces]
        )
        split = products.reshape(2, 2, half, products.shape[-1])
        keep = lax.dynamic_index_in_dim(split, low, 1, keepdims=False)
        send = lax.dynamic_index_in_dim(split, 1 - low, 1, keepdims=False)
        return keep + lax.ppermute(send, "tp", tp_pairs(1))

    def second_halving(summed):
        chosen = here % 2 ^ middle
        keep = lax.dynamic_index_in_dim(summed, chosen, 0, keepdims=False)
        send = lax.dynamic_index_in_dim(summed, 1 - chosen, 0, keepdims=False)
        return keep + lax.ppermute(send, "tp", tp_pairs(2))

    near = second_halving(first_halving((block, across_x)))
    far_summed = first_halving((across_y, diagonal))
    columns = near.shape[-1]
    width = columns // 2
    chosen = here // 2 % 2 ^ high
    results = []
    previous = None
    for start in (0, width):
        piece = far_summed[..., start : start + width]
        if previous is not None:
            _, piece = lax.optimization_barrier((previous, piece))
        far = second_halving(piece)
        both = jnp.stack([near[:, start : start + width], far])
        keep = lax.dynamic_index_in_dim(both, chosen, 0, keepdims=False)
        send = lax.dynamic_index_in_dim(both, 1 - chosen, 0, keepdims=False)
        results.append(keep + lax.ppermute(send, "tp", tp_pairs(4)))
        previous = far
    return jnp.concatenate(results, axis=1)


def shards(hidden, down_weight, channel_scale):
    seq_count = lax.axis_size("seq")
    tp_count = lax.axis_size("tp")
    tokens, units = hidden.shape
    groups = tp_count // seq_count
    owned = tokens // groups
    piece = owned // CHUNKS
    grouped = hidden.reshape(groups, CHUNKS, piece, units)
    outputs = []
    for chunk in range(CHUNKS):
        part = grouped[:, chunk].reshape(groups * piece, units)
        if tp_count == 8:
            rotated = spread_rotate_return(part)
        else:
            spread = lax.all_to_all(part, "tp", split_axis=0, concat_axis=1, tiled=True)
            turned = rotate(spread)
            rotated = lax.all_to_all(turned, "tp", split_axis=1, concat_axis=0, tiled=True)
        if seq_count == 4 and tp_count == 8:
            outputs.append(product_and_reduce(rotated, down_weight))
        else:
            partial_terms = gathered_product(rotated, down_weight)
            outputs.append(scatter_sum_tp(partial_terms))
    summed = jnp.concatenate(outputs, axis=0)
    return (summed * channel_scale[None, :]).astype(jnp.bfloat16)


def solution(mesh):
    placed = (P("seq", "tp"), P("tp", "seq"), P("seq"))
    return jax.shard_map(
        shards, mesh=mesh, in_specs=placed, out_specs=P("tp", "seq"), check_vma=False
    )
```

```python
import math

import jax
import jax.numpy as jnp
import numpy as np
from jax import lax
from jax.sharding import PartitionSpec as P

PALEY = 28
INNER = 32
CHUNKS = 1
TAIL_PIECES = 4


def paley_table():
    residues = set((value * value % 13 for value in range(1, 13)))
    conference = np.zeros((14, 14))
    conference[0, 1:] = 1.0
    conference[1:, 0] = 1.0
    for first in range(13):
        for second in range(13):
            gap = (second - first) % 13
            if gap != 0:
                conference[1 + first, 1 + second] = 1.0 if gap in residues else -1.0
    upper = np.array([[1.0, 1.0], [1.0, -1.0]])
    lower = np.array([[1.0, -1.0], [-1.0, -1.0]])
    return np.kron(conference, upper) + np.kron(np.eye(14), lower)


def walsh_table(order):
    index_rows = np.arange(order)[:, None]
    index_cols = np.arange(order)[None, :]
    signs = np.ones((order, order))
    bit_value = 1
    while bit_value < order:
        both_set = index_rows // bit_value % 2 * (index_cols // bit_value % 2)
        signs = signs * (1 - 2 * both_set)
        bit_value = bit_value * 2
    return signs


def rotate(spread):
    rows, total_units = spread.shape
    walsh = total_units // PALEY
    outer_order = walsh // INNER
    width = INNER * PALEY
    inner_table = jnp.asarray(np.kron(walsh_table(INNER), paley_table()), jnp.bfloat16)
    outer_table = jnp.asarray(walsh_table(outer_order), jnp.float32)
    blocks = spread.reshape(rows, outer_order, width)
    inner = jnp.einsum("rbl,lm->rbm", blocks, inner_table, preferred_element_type=jnp.float32)
    outer = jnp.einsum("rbm,bc->rcm", inner, outer_table, precision=lax.Precision.HIGHEST)
    factor = 1.0 / math.sqrt(total_units)
    return (outer * factor).astype(jnp.bfloat16).reshape(rows, total_units)


def gathered_product(block, down_weight):
    seq_count = lax.axis_size("seq")
    if seq_count != 4:
        gathered = lax.all_gather(block, "seq", axis=0, tiled=True)
        return jnp.dot(gathered, down_weight, preferred_element_type=jnp.float32)
    rows = block.shape[0]
    half = rows // 2
    across_x = lax.ppermute(block, "seq", [(s, s ^ 1) for s in range(4)])
    across_y = lax.ppermute(block, "seq", [(s, s ^ 2) for s in range(4)])
    first = lax.ppermute(across_y[:half], "seq", [(s, s ^ 1) for s in range(4)])
    second = lax.ppermute(across_x[half:], "seq", [(s, s ^ 2) for s in range(4)])
    diagonal = jnp.concatenate([first, second], axis=0)
    me = lax.axis_index("seq")
    columns = down_weight.shape[1]
    result = jnp.zeros((4 * rows, columns), jnp.float32)
    for other, piece in enumerate((block, across_x, across_y, diagonal)):
        product = jnp.dot(piece, down_weight, preferred_element_type=jnp.float32)
        result = lax.dynamic_update_slice_in_dim(result, product, (me ^ other) * rows, 0)
    return result


def scatter_sum_tp(partial_terms):
    tp_count = lax.axis_size("tp")
    if tp_count != 8:
        return lax.psum_scatter(partial_terms, "tp", scatter_dimension=0, tiled=True)
    rows, columns = partial_terms.shape
    share = rows // tp_count
    me = lax.axis_index("tp")
    pairs = lambda distance: [(k, k ^ distance) for k in range(tp_count)]
    blocks = partial_terms.reshape(2, 2, 2, share, columns)
    low = me % 2
    keep = lax.dynamic_index_in_dim(blocks, low, 2, keepdims=False)
    send = lax.dynamic_index_in_dim(blocks, 1 - low, 2, keepdims=False)
    summed = keep + lax.ppermute(send, "tp", pairs(1))
    middle = me // 2 % 2
    keep = lax.dynamic_index_in_dim(summed, middle, 1, keepdims=False)
    send = lax.dynamic_index_in_dim(summed, 1 - middle, 1, keepdims=False)
    summed = keep + lax.ppermute(send, "tp", pairs(2))
    high = me // 4 % 2
    keep = lax.dynamic_index_in_dim(summed, high, 0, keepdims=False)
    send = lax.dynamic_index_in_dim(summed, 1 - high, 0, keepdims=False)
    return keep + lax.ppermute(send, "tp", pairs(4))


def spread_rotate_return(part):
    tp_count = lax.axis_size("tp")
    rows, units = part.shape
    share = rows // tp_count
    width = INNER * PALEY
    sub = units // width
    me = lax.axis_index("tp")
    pairs = lambda distance: [(k, k ^ distance) for k in range(tp_count)]
    inner_table = jnp.asarray(np.kron(walsh_table(INNER), paley_table()), jnp.bfloat16)
    landed = []
    for distance in range(tp_count):
        send = lax.dynamic_slice_in_dim(part, (me ^ distance) * share, share, 0)
        if distance:
            send = lax.ppermute(send, "tp", pairs(distance))
        landed.append(
            jnp.einsum(
                "rbl,lm->rbm",
                send.reshape(share, sub, width),
                inner_table,
                preferred_element_type=jnp.float32,
            )
        )
    inner = jnp.stack(landed, axis=1).reshape(share, tp_count * sub, width)
    order = jnp.arange(tp_count, dtype=jnp.int32)
    source = me ^ order
    signs = 1 - 2 * (lax.population_count(source[:, None] & source[None, :]) % 2)
    mixing = jnp.kron(signs.astype(jnp.float32), jnp.asarray(walsh_table(sub), jnp.float32))
    outer = jnp.einsum("rbm,bc->rcm", inner, mixing, precision=lax.Precision.HIGHEST)
    factor = 1.0 / math.sqrt(units * tp_count)
    turned = (outer * factor).astype(jnp.bfloat16).reshape(share, tp_count, units)
    result = jnp.zeros((rows, units), jnp.bfloat16)
    for distance in range(tp_count):
        block = turned[:, distance]
        if distance:
            block = lax.ppermute(block, "tp", pairs(distance))
        result = lax.dynamic_update_slice_in_dim(result, block, (me ^ distance) * share, 0)
    return result


def product_and_reduce(block, down_weight):
    rows = block.shape[0]
    half = rows // 2
    seq_pairs = lambda distance: [(s, s ^ distance) for s in range(4)]
    tp_pairs = lambda distance: [(k, k ^ distance) for k in range(8)]
    here = lax.axis_index("seq")
    me = lax.axis_index("tp")
    low, middle, high = me % 2, me // 2 % 2, me // 4 % 2
    across_x = lax.ppermute(block, "seq", seq_pairs(1))
    across_y = lax.ppermute(block, "seq", seq_pairs(2))
    first = lax.ppermute(across_y[:half], "seq", seq_pairs(1))
    second = lax.ppermute(across_x[half:], "seq", seq_pairs(2))
    diagonal = jnp.concatenate([first, second], axis=0)

    def first_halving(pieces):
        products = jnp.stack(
            [jnp.dot(piece, down_weight, preferred_element_type=jnp.float32) for piece in pieces]
        )
        split = products.reshape(2, 2, half, products.shape[-1])
        keep = lax.dynamic_index_in_dim(split, low, 1, keepdims=False)
        send = lax.dynamic_index_in_dim(split, 1 - low, 1, keepdims=False)
        return keep + lax.ppermute(send, "tp", tp_pairs(1))

    def second_halving(summed):
        chosen = here % 2 ^ middle
        keep = lax.dynamic_index_in_dim(summed, chosen, 0, keepdims=False)
        send = lax.dynamic_index_in_dim(summed, 1 - chosen, 0, keepdims=False)
        return keep + lax.ppermute(send, "tp", tp_pairs(2))

    near = second_halving(first_halving((block, across_x)))
    far_summed = first_halving((across_y, diagonal))
    columns = near.shape[-1]
    width = columns // TAIL_PIECES
    chosen = here // 2 % 2 ^ high
    results = []
    previous = None
    for start in range(0, columns, width):
        piece = far_summed[..., start : start + width]
        if previous is not None:
            _, piece = lax.optimization_barrier((previous, piece))
        far = second_halving(piece)
        both = jnp.stack([near[:, start : start + width], far])
        keep = lax.dynamic_index_in_dim(both, chosen, 0, keepdims=False)
        send = lax.dynamic_index_in_dim(both, 1 - chosen, 0, keepdims=False)
        results.append(keep + lax.ppermute(send, "tp", tp_pairs(4)))
        previous = far
    return jnp.concatenate(results, axis=1)


def shards(hidden, down_weight, channel_scale):
    seq_count = lax.axis_size("seq")
    tp_count = lax.axis_size("tp")
    tokens, units = hidden.shape
    groups = tp_count // seq_count
    owned = tokens // groups
    piece = owned // CHUNKS
    grouped = hidden.reshape(groups, CHUNKS, piece, units)
    outputs = []
    for chunk in range(CHUNKS):
        part = grouped[:, chunk].reshape(groups * piece, units)
        if tp_count == 8:
            rotated = spread_rotate_return(part)
        else:
            spread = lax.all_to_all(part, "tp", split_axis=0, concat_axis=1, tiled=True)
            turned = rotate(spread)
            rotated = lax.all_to_all(turned, "tp", split_axis=1, concat_axis=0, tiled=True)
        if seq_count == 4 and tp_count == 8:
            outputs.append(product_and_reduce(rotated, down_weight))
        else:
            partial_terms = gathered_product(rotated, down_weight)
            outputs.append(scatter_sum_tp(partial_terms))
    summed = jnp.concatenate(outputs, axis=0)
    return (summed * channel_scale[None, :]).astype(jnp.bfloat16)


def solution(mesh):
    placed = (P("seq", "tp"), P("tp", "seq"), P("seq"))
    return jax.shard_map(
        shards, mesh=mesh, in_specs=placed, out_specs=P("tp", "seq"), check_vma=False
    )
```

```python
import math

import jax
import jax.numpy as jnp
import numpy as np
from jax import lax
from jax.sharding import PartitionSpec as P

PALEY = 28
INNER = 32
CHUNKS = 1
TAIL_PIECES = 4


def paley_table():
    residues = set((value * value % 13 for value in range(1, 13)))
    conference = np.zeros((14, 14))
    conference[0, 1:] = 1.0
    conference[1:, 0] = 1.0
    for first in range(13):
        for second in range(13):
            gap = (second - first) % 13
            if gap != 0:
                conference[1 + first, 1 + second] = 1.0 if gap in residues else -1.0
    upper = np.array([[1.0, 1.0], [1.0, -1.0]])
    lower = np.array([[1.0, -1.0], [-1.0, -1.0]])
    return np.kron(conference, upper) + np.kron(np.eye(14), lower)


def walsh_table(order):
    index_rows = np.arange(order)[:, None]
    index_cols = np.arange(order)[None, :]
    signs = np.ones((order, order))
    bit_value = 1
    while bit_value < order:
        both_set = index_rows // bit_value % 2 * (index_cols // bit_value % 2)
        signs = signs * (1 - 2 * both_set)
        bit_value = bit_value * 2
    return signs


def rotate(spread):
    rows, total_units = spread.shape
    walsh = total_units // PALEY
    outer_order = walsh // INNER
    width = INNER * PALEY
    inner_table = jnp.asarray(np.kron(walsh_table(INNER), paley_table()), jnp.bfloat16)
    outer_table = jnp.asarray(walsh_table(outer_order), jnp.float32)
    blocks = spread.reshape(rows, outer_order, width)
    inner = jnp.einsum("rbl,lm->rbm", blocks, inner_table, preferred_element_type=jnp.float32)
    outer = jnp.einsum("rbm,bc->rcm", inner, outer_table, precision=lax.Precision.HIGHEST)
    factor = 1.0 / math.sqrt(total_units)
    return (outer * factor).astype(jnp.bfloat16).reshape(rows, total_units)


def gathered_product(block, down_weight):
    seq_count = lax.axis_size("seq")
    if seq_count != 4:
        gathered = lax.all_gather(block, "seq", axis=0, tiled=True)
        return jnp.dot(gathered, down_weight, preferred_element_type=jnp.float32)
    rows = block.shape[0]
    half = rows // 2
    across_x = lax.ppermute(block, "seq", [(s, s ^ 1) for s in range(4)])
    across_y = lax.ppermute(block, "seq", [(s, s ^ 2) for s in range(4)])
    first = lax.ppermute(across_y[:half], "seq", [(s, s ^ 1) for s in range(4)])
    second = lax.ppermute(across_x[half:], "seq", [(s, s ^ 2) for s in range(4)])
    diagonal = jnp.concatenate([first, second], axis=0)
    me = lax.axis_index("seq")
    columns = down_weight.shape[1]
    result = jnp.zeros((4 * rows, columns), jnp.float32)
    for other, piece in enumerate((block, across_x, across_y, diagonal)):
        product = jnp.dot(piece, down_weight, preferred_element_type=jnp.float32)
        result = lax.dynamic_update_slice_in_dim(result, product, (me ^ other) * rows, 0)
    return result


def scatter_sum_tp(partial_terms):
    tp_count = lax.axis_size("tp")
    if tp_count != 8:
        return lax.psum_scatter(partial_terms, "tp", scatter_dimension=0, tiled=True)
    rows, columns = partial_terms.shape
    share = rows // tp_count
    me = lax.axis_index("tp")
    pairs = lambda distance: [(k, k ^ distance) for k in range(tp_count)]
    blocks = partial_terms.reshape(2, 2, 2, share, columns)
    low = me % 2
    keep = lax.dynamic_index_in_dim(blocks, low, 2, keepdims=False)
    send = lax.dynamic_index_in_dim(blocks, 1 - low, 2, keepdims=False)
    summed = keep + lax.ppermute(send, "tp", pairs(1))
    middle = me // 2 % 2
    keep = lax.dynamic_index_in_dim(summed, middle, 1, keepdims=False)
    send = lax.dynamic_index_in_dim(summed, 1 - middle, 1, keepdims=False)
    summed = keep + lax.ppermute(send, "tp", pairs(2))
    high = me // 4 % 2
    keep = lax.dynamic_index_in_dim(summed, high, 0, keepdims=False)
    send = lax.dynamic_index_in_dim(summed, 1 - high, 0, keepdims=False)
    return keep + lax.ppermute(send, "tp", pairs(4))


def spread_rotate_return(part):
    tp_count = lax.axis_size("tp")
    rows, units = part.shape
    share = rows // tp_count
    width = INNER * PALEY
    sub = units // width
    me = lax.axis_index("tp")
    pairs = lambda distance: [(k, k ^ distance) for k in range(tp_count)]
    inner_table = jnp.asarray(np.kron(walsh_table(INNER), paley_table()), jnp.bfloat16)
    landed = []
    for distance in range(tp_count):
        send = lax.dynamic_slice_in_dim(part, (me ^ distance) * share, share, 0)
        if distance:
            send = lax.ppermute(send, "tp", pairs(distance))
        landed.append(
            jnp.einsum(
                "rbl,lm->rbm",
                send.reshape(share, sub, width),
                inner_table,
                preferred_element_type=jnp.float32,
            )
        )
    inner = jnp.stack(landed, axis=1).reshape(share, tp_count * sub, width)
    order = jnp.arange(tp_count, dtype=jnp.int32)
    source = me ^ order
    signs = 1 - 2 * (lax.population_count(source[:, None] & source[None, :]) % 2)
    mixing = jnp.kron(signs.astype(jnp.float32), jnp.asarray(walsh_table(sub), jnp.float32))
    outer = jnp.einsum("rbm,bc->rcm", inner, mixing, precision=lax.Precision.HIGHEST)
    factor = 1.0 / math.sqrt(units * tp_count)
    turned = (outer * factor).astype(jnp.bfloat16).reshape(share, tp_count, units)
    result = jnp.zeros((rows, units), jnp.bfloat16)
    for distance in range(tp_count):
        block = turned[:, distance]
        if distance:
            block = lax.ppermute(block, "tp", pairs(distance))
        result = lax.dynamic_update_slice_in_dim(result, block, (me ^ distance) * share, 0)
    return result


def product_and_reduce(block, down_weight):
    rows = block.shape[0]
    half = rows // 2
    seq_pairs = lambda distance: [(s, s ^ distance) for s in range(4)]
    tp_pairs = lambda distance: [(k, k ^ distance) for k in range(8)]
    here = lax.axis_index("seq")
    me = lax.axis_index("tp")
    low, middle, high = me % 2, me // 2 % 2, me // 4 % 2
    across_x = lax.ppermute(block, "seq", seq_pairs(1))
    across_y = lax.ppermute(block, "seq", seq_pairs(2))
    first = lax.ppermute(across_y[:half], "seq", seq_pairs(1))
    second = lax.ppermute(across_x[half:], "seq", seq_pairs(2))
    diagonal = jnp.concatenate([first, second], axis=0)

    def first_halving(pieces, weight=down_weight):
        products = jnp.stack(
            [jnp.dot(piece, weight, preferred_element_type=jnp.float32) for piece in pieces]
        )
        split = products.reshape(2, 2, half, products.shape[-1])
        keep = lax.dynamic_index_in_dim(split, low, 1, keepdims=False)
        send = lax.dynamic_index_in_dim(split, 1 - low, 1, keepdims=False)
        return keep + lax.ppermute(send, "tp", tp_pairs(1))

    def second_halving(summed):
        chosen = here % 2 ^ middle
        keep = lax.dynamic_index_in_dim(summed, chosen, 0, keepdims=False)
        send = lax.dynamic_index_in_dim(summed, 1 - chosen, 0, keepdims=False)
        return keep + lax.ppermute(send, "tp", tp_pairs(2))

    near_width = down_weight.shape[1] // 2
    near_parts = []
    for start in (0, near_width):
        summed = first_halving((block, across_x), down_weight[:, start : start + near_width])
        near_parts.append(second_halving(summed))
    near = jnp.concatenate(near_parts, axis=1)
    far_summed = first_halving((across_y, diagonal))
    columns = near.shape[-1]
    width = columns // TAIL_PIECES
    chosen = here // 2 % 2 ^ high
    results = []
    previous = None
    for start in range(0, columns, width):
        piece = far_summed[..., start : start + width]
        if previous is not None:
            _, piece = lax.optimization_barrier((previous, piece))
        far = second_halving(piece)
        both = jnp.stack([near[:, start : start + width], far])
        keep = lax.dynamic_index_in_dim(both, chosen, 0, keepdims=False)
        send = lax.dynamic_index_in_dim(both, 1 - chosen, 0, keepdims=False)
        results.append(keep + lax.ppermute(send, "tp", tp_pairs(4)))
        previous = far
    return jnp.concatenate(results, axis=1)


def shards(hidden, down_weight, channel_scale):
    seq_count = lax.axis_size("seq")
    tp_count = lax.axis_size("tp")
    tokens, units = hidden.shape
    groups = tp_count // seq_count
    owned = tokens // groups
    piece = owned // CHUNKS
    grouped = hidden.reshape(groups, CHUNKS, piece, units)
    outputs = []
    for chunk in range(CHUNKS):
        part = grouped[:, chunk].reshape(groups * piece, units)
        if tp_count == 8:
            rotated = spread_rotate_return(part)
        else:
            spread = lax.all_to_all(part, "tp", split_axis=0, concat_axis=1, tiled=True)
            turned = rotate(spread)
            rotated = lax.all_to_all(turned, "tp", split_axis=1, concat_axis=0, tiled=True)
        if seq_count == 4 and tp_count == 8:
            outputs.append(product_and_reduce(rotated, down_weight))
        else:
            partial_terms = gathered_product(rotated, down_weight)
            outputs.append(scatter_sum_tp(partial_terms))
    summed = jnp.concatenate(outputs, axis=0)
    return (summed * channel_scale[None, :]).astype(jnp.bfloat16)


def solution(mesh):
    placed = (P("seq", "tp"), P("tp", "seq"), P("seq"))
    return jax.shard_map(
        shards, mesh=mesh, in_specs=placed, out_specs=P("tp", "seq"), check_vma=False
    )
```

```python
import math

import jax
import jax.numpy as jnp
import numpy as np
from jax import lax
from jax.sharding import PartitionSpec as P

PALEY = 28
INNER = 32
CHUNKS = 1
TAIL_PIECES = 4


def paley_table():
    residues = set((value * value % 13 for value in range(1, 13)))
    conference = np.zeros((14, 14))
    conference[0, 1:] = 1.0
    conference[1:, 0] = 1.0
    for first in range(13):
        for second in range(13):
            gap = (second - first) % 13
            if gap != 0:
                conference[1 + first, 1 + second] = 1.0 if gap in residues else -1.0
    upper = np.array([[1.0, 1.0], [1.0, -1.0]])
    lower = np.array([[1.0, -1.0], [-1.0, -1.0]])
    return np.kron(conference, upper) + np.kron(np.eye(14), lower)


def walsh_table(order):
    index_rows = np.arange(order)[:, None]
    index_cols = np.arange(order)[None, :]
    signs = np.ones((order, order))
    bit_value = 1
    while bit_value < order:
        both_set = index_rows // bit_value % 2 * (index_cols // bit_value % 2)
        signs = signs * (1 - 2 * both_set)
        bit_value = bit_value * 2
    return signs


def rotate(spread):
    rows, total_units = spread.shape
    walsh = total_units // PALEY
    outer_order = walsh // INNER
    width = INNER * PALEY
    inner_table = jnp.asarray(np.kron(walsh_table(INNER), paley_table()), jnp.bfloat16)
    outer_table = jnp.asarray(walsh_table(outer_order), jnp.float32)
    blocks = spread.reshape(rows, outer_order, width)
    inner = jnp.einsum("rbl,lm->rbm", blocks, inner_table, preferred_element_type=jnp.float32)
    outer = jnp.einsum("rbm,bc->rcm", inner, outer_table, precision=lax.Precision.HIGHEST)
    factor = 1.0 / math.sqrt(total_units)
    return (outer * factor).astype(jnp.bfloat16).reshape(rows, total_units)


def gathered_product(block, down_weight):
    seq_count = lax.axis_size("seq")
    if seq_count != 4:
        gathered = lax.all_gather(block, "seq", axis=0, tiled=True)
        return jnp.dot(gathered, down_weight, preferred_element_type=jnp.float32)
    rows = block.shape[0]
    half = rows // 2
    across_x = lax.ppermute(block, "seq", [(s, s ^ 1) for s in range(4)])
    across_y = lax.ppermute(block, "seq", [(s, s ^ 2) for s in range(4)])
    first = lax.ppermute(across_y[:half], "seq", [(s, s ^ 1) for s in range(4)])
    second = lax.ppermute(across_x[half:], "seq", [(s, s ^ 2) for s in range(4)])
    diagonal = jnp.concatenate([first, second], axis=0)
    me = lax.axis_index("seq")
    columns = down_weight.shape[1]
    result = jnp.zeros((4 * rows, columns), jnp.float32)
    for other, piece in enumerate((block, across_x, across_y, diagonal)):
        product = jnp.dot(piece, down_weight, preferred_element_type=jnp.float32)
        result = lax.dynamic_update_slice_in_dim(result, product, (me ^ other) * rows, 0)
    return result


def scatter_sum_tp(partial_terms):
    tp_count = lax.axis_size("tp")
    if tp_count != 8:
        return lax.psum_scatter(partial_terms, "tp", scatter_dimension=0, tiled=True)
    rows, columns = partial_terms.shape
    share = rows // tp_count
    me = lax.axis_index("tp")
    pairs = lambda distance: [(k, k ^ distance) for k in range(tp_count)]
    blocks = partial_terms.reshape(2, 2, 2, share, columns)
    low = me % 2
    keep = lax.dynamic_index_in_dim(blocks, low, 2, keepdims=False)
    send = lax.dynamic_index_in_dim(blocks, 1 - low, 2, keepdims=False)
    summed = keep + lax.ppermute(send, "tp", pairs(1))
    middle = me // 2 % 2
    keep = lax.dynamic_index_in_dim(summed, middle, 1, keepdims=False)
    send = lax.dynamic_index_in_dim(summed, 1 - middle, 1, keepdims=False)
    summed = keep + lax.ppermute(send, "tp", pairs(2))
    high = me // 4 % 2
    keep = lax.dynamic_index_in_dim(summed, high, 0, keepdims=False)
    send = lax.dynamic_index_in_dim(summed, 1 - high, 0, keepdims=False)
    return keep + lax.ppermute(send, "tp", pairs(4))


def spread_rotate_return(part):
    tp_count = lax.axis_size("tp")
    rows, units = part.shape
    share = rows // tp_count
    width = INNER * PALEY
    sub = units // width
    me = lax.axis_index("tp")
    pairs = lambda distance: [(k, k ^ distance) for k in range(tp_count)]
    inner_table = jnp.asarray(np.kron(walsh_table(INNER), paley_table()), jnp.bfloat16)
    landed = []
    for distance in range(tp_count):
        send = lax.dynamic_slice_in_dim(part, (me ^ distance) * share, share, 0)
        if distance:
            send = lax.ppermute(send, "tp", pairs(distance))
        landed.append(
            jnp.einsum(
                "rbl,lm->rbm",
                send.reshape(share, sub, width),
                inner_table,
                preferred_element_type=jnp.float32,
            )
        )
    inner = jnp.stack(landed, axis=1).reshape(share, tp_count * sub, width)
    order = jnp.arange(tp_count, dtype=jnp.int32)
    source = me ^ order
    signs = 1 - 2 * (lax.population_count(source[:, None] & source[None, :]) % 2)
    mixing = jnp.kron(signs.astype(jnp.float32), jnp.asarray(walsh_table(sub), jnp.float32))
    outer = jnp.einsum("rbm,bc->rcm", inner, mixing, precision=lax.Precision.HIGHEST)
    factor = 1.0 / math.sqrt(units * tp_count)
    turned = (outer * factor).astype(jnp.bfloat16).reshape(share, tp_count, units)
    result = jnp.zeros((rows, units), jnp.bfloat16)
    for distance in range(tp_count):
        block = turned[:, distance]
        if distance:
            block = lax.ppermute(block, "tp", pairs(distance))
        result = lax.dynamic_update_slice_in_dim(result, block, (me ^ distance) * share, 0)
    return result


def product_and_reduce(block, down_weight):
    rows = block.shape[0]
    half = rows // 2
    seq_pairs = lambda distance: [(s, s ^ distance) for s in range(4)]
    tp_pairs = lambda distance: [(k, k ^ distance) for k in range(8)]
    here = lax.axis_index("seq")
    me = lax.axis_index("tp")
    low, middle, high = me % 2, me // 2 % 2, me // 4 % 2
    across_x = lax.ppermute(block, "seq", seq_pairs(1))
    across_y = lax.ppermute(block, "seq", seq_pairs(2))
    first = lax.ppermute(across_y[:half], "seq", seq_pairs(1))
    second = lax.ppermute(across_x[half:], "seq", seq_pairs(2))
    diagonal = jnp.concatenate([first, second], axis=0)

    def multiply(pieces):
        return jnp.stack(
            [jnp.dot(piece, down_weight, preferred_element_type=jnp.float32) for piece in pieces]
        )

    def first_halving(products):
        split = products.reshape(2, 2, half, products.shape[-1])
        keep = lax.dynamic_index_in_dim(split, low, 1, keepdims=False)
        send = lax.dynamic_index_in_dim(split, 1 - low, 1, keepdims=False)
        return keep + lax.ppermute(send, "tp", tp_pairs(1))

    def second_halving(summed):
        chosen = here % 2 ^ middle
        keep = lax.dynamic_index_in_dim(summed, chosen, 0, keepdims=False)
        send = lax.dynamic_index_in_dim(summed, 1 - chosen, 0, keepdims=False)
        return keep + lax.ppermute(send, "tp", tp_pairs(2))

    near = second_halving(first_halving(multiply((block, across_x))))
    far_products = multiply((across_y, diagonal))
    columns = near.shape[-1]
    width = columns // TAIL_PIECES
    chosen = here // 2 % 2 ^ high
    results = []
    previous = None
    for start in range(0, columns, width):
        piece = first_halving(far_products[..., start : start + width])
        if previous is not None:
            _, piece = lax.optimization_barrier((previous, piece))
        far = second_halving(piece)
        both = jnp.stack([near[:, start : start + width], far])
        keep = lax.dynamic_index_in_dim(both, chosen, 0, keepdims=False)
        send = lax.dynamic_index_in_dim(both, 1 - chosen, 0, keepdims=False)
        results.append(keep + lax.ppermute(send, "tp", tp_pairs(4)))
        previous = far
    return jnp.concatenate(results, axis=1)


def shards(hidden, down_weight, channel_scale):
    seq_count = lax.axis_size("seq")
    tp_count = lax.axis_size("tp")
    tokens, units = hidden.shape
    groups = tp_count // seq_count
    owned = tokens // groups
    piece = owned // CHUNKS
    grouped = hidden.reshape(groups, CHUNKS, piece, units)
    outputs = []
    for chunk in range(CHUNKS):
        part = grouped[:, chunk].reshape(groups * piece, units)
        if tp_count == 8:
            rotated = spread_rotate_return(part)
        else:
            spread = lax.all_to_all(part, "tp", split_axis=0, concat_axis=1, tiled=True)
            turned = rotate(spread)
            rotated = lax.all_to_all(turned, "tp", split_axis=1, concat_axis=0, tiled=True)
        if seq_count == 4 and tp_count == 8:
            outputs.append(product_and_reduce(rotated, down_weight))
        else:
            partial_terms = gathered_product(rotated, down_weight)
            outputs.append(scatter_sum_tp(partial_terms))
    summed = jnp.concatenate(outputs, axis=0)
    return (summed * channel_scale[None, :]).astype(jnp.bfloat16)


def solution(mesh):
    placed = (P("seq", "tp"), P("tp", "seq"), P("seq"))
    return jax.shard_map(
        shards, mesh=mesh, in_specs=placed, out_specs=P("tp", "seq"), check_vma=False
    )
```

```python
import math

import jax
import jax.numpy as jnp
import numpy as np
from jax import lax
from jax.sharding import PartitionSpec as P

PALEY = 28
INNER = 32
CHUNKS = 1
TAIL_PIECES = 4


def paley_table():
    residues = set((value * value % 13 for value in range(1, 13)))
    conference = np.zeros((14, 14))
    conference[0, 1:] = 1.0
    conference[1:, 0] = 1.0
    for first in range(13):
        for second in range(13):
            gap = (second - first) % 13
            if gap != 0:
                conference[1 + first, 1 + second] = 1.0 if gap in residues else -1.0
    upper = np.array([[1.0, 1.0], [1.0, -1.0]])
    lower = np.array([[1.0, -1.0], [-1.0, -1.0]])
    return np.kron(conference, upper) + np.kron(np.eye(14), lower)


def walsh_table(order):
    index_rows = np.arange(order)[:, None]
    index_cols = np.arange(order)[None, :]
    signs = np.ones((order, order))
    bit_value = 1
    while bit_value < order:
        both_set = index_rows // bit_value % 2 * (index_cols // bit_value % 2)
        signs = signs * (1 - 2 * both_set)
        bit_value = bit_value * 2
    return signs


def rotate(spread):
    rows, total_units = spread.shape
    walsh = total_units // PALEY
    outer_order = walsh // INNER
    width = INNER * PALEY
    inner_table = jnp.asarray(np.kron(walsh_table(INNER), paley_table()), jnp.bfloat16)
    outer_table = jnp.asarray(walsh_table(outer_order), jnp.float32)
    blocks = spread.reshape(rows, outer_order, width)
    inner = jnp.einsum("rbl,lm->rbm", blocks, inner_table, preferred_element_type=jnp.float32)
    outer = jnp.einsum("rbm,bc->rcm", inner, outer_table, precision=lax.Precision.HIGHEST)
    factor = 1.0 / math.sqrt(total_units)
    return (outer * factor).astype(jnp.bfloat16).reshape(rows, total_units)


def gathered_product(block, down_weight):
    seq_count = lax.axis_size("seq")
    if seq_count != 4:
        gathered = lax.all_gather(block, "seq", axis=0, tiled=True)
        return jnp.dot(gathered, down_weight, preferred_element_type=jnp.float32)
    rows = block.shape[0]
    half = rows // 2
    across_x = lax.ppermute(block, "seq", [(s, s ^ 1) for s in range(4)])
    across_y = lax.ppermute(block, "seq", [(s, s ^ 2) for s in range(4)])
    first = lax.ppermute(across_y[:half], "seq", [(s, s ^ 1) for s in range(4)])
    second = lax.ppermute(across_x[half:], "seq", [(s, s ^ 2) for s in range(4)])
    diagonal = jnp.concatenate([first, second], axis=0)
    me = lax.axis_index("seq")
    columns = down_weight.shape[1]
    result = jnp.zeros((4 * rows, columns), jnp.float32)
    for other, piece in enumerate((block, across_x, across_y, diagonal)):
        product = jnp.dot(piece, down_weight, preferred_element_type=jnp.float32)
        result = lax.dynamic_update_slice_in_dim(result, product, (me ^ other) * rows, 0)
    return result


def scatter_sum_tp(partial_terms):
    tp_count = lax.axis_size("tp")
    if tp_count != 8:
        return lax.psum_scatter(partial_terms, "tp", scatter_dimension=0, tiled=True)
    rows, columns = partial_terms.shape
    share = rows // tp_count
    me = lax.axis_index("tp")
    pairs = lambda distance: [(k, k ^ distance) for k in range(tp_count)]
    blocks = partial_terms.reshape(2, 2, 2, share, columns)
    low = me % 2
    keep = lax.dynamic_index_in_dim(blocks, low, 2, keepdims=False)
    send = lax.dynamic_index_in_dim(blocks, 1 - low, 2, keepdims=False)
    summed = keep + lax.ppermute(send, "tp", pairs(1))
    middle = me // 2 % 2
    keep = lax.dynamic_index_in_dim(summed, middle, 1, keepdims=False)
    send = lax.dynamic_index_in_dim(summed, 1 - middle, 1, keepdims=False)
    summed = keep + lax.ppermute(send, "tp", pairs(2))
    high = me // 4 % 2
    keep = lax.dynamic_index_in_dim(summed, high, 0, keepdims=False)
    send = lax.dynamic_index_in_dim(summed, 1 - high, 0, keepdims=False)
    return keep + lax.ppermute(send, "tp", pairs(4))


def spread_rotate_return(part):
    tp_count = lax.axis_size("tp")
    rows, units = part.shape
    share = rows // tp_count
    width = INNER * PALEY
    sub = units // width
    me = lax.axis_index("tp")
    pairs = lambda distance: [(k, k ^ distance) for k in range(tp_count)]
    inner_table = jnp.asarray(np.kron(walsh_table(INNER), paley_table()), jnp.bfloat16)
    landed = []
    for distance in range(tp_count):
        send = lax.dynamic_slice_in_dim(part, (me ^ distance) * share, share, 0)
        if distance:
            send = lax.ppermute(send, "tp", pairs(distance))
        landed.append(
            jnp.einsum(
                "rbl,lm->rbm",
                send.reshape(share, sub, width),
                inner_table,
                preferred_element_type=jnp.float32,
            )
        )
    inner = jnp.stack(landed, axis=1).reshape(share, tp_count * sub, width)
    order = jnp.arange(tp_count, dtype=jnp.int32)
    source = me ^ order
    signs = 1 - 2 * (lax.population_count(source[:, None] & source[None, :]) % 2)
    mixing = jnp.kron(signs.astype(jnp.float32), jnp.asarray(walsh_table(sub), jnp.float32))
    outer = jnp.einsum("rbm,bc->rcm", inner, mixing, precision=lax.Precision.HIGHEST)
    factor = 1.0 / math.sqrt(units * tp_count)
    turned = (outer * factor).astype(jnp.bfloat16).reshape(share, tp_count, units)
    result = jnp.zeros((rows, units), jnp.bfloat16)
    for distance in range(tp_count):
        block = turned[:, distance]
        if distance:
            block = lax.ppermute(block, "tp", pairs(distance))
        result = lax.dynamic_update_slice_in_dim(result, block, (me ^ distance) * share, 0)
    return result


def product_and_reduce(block, down_weight):
    rows = block.shape[0]
    half = rows // 2
    seq_pairs = lambda distance: [(s, s ^ distance) for s in range(4)]
    tp_pairs = lambda distance: [(k, k ^ distance) for k in range(8)]
    here = lax.axis_index("seq")
    me = lax.axis_index("tp")
    low, middle, high = me % 2, me // 2 % 2, me // 4 % 2
    across_x = lax.ppermute(block, "seq", seq_pairs(1))
    across_y = lax.ppermute(block, "seq", seq_pairs(2))
    first = lax.ppermute(across_y[:half], "seq", seq_pairs(1))
    second = lax.ppermute(across_x[half:], "seq", seq_pairs(2))
    diagonal = jnp.concatenate([first, second], axis=0)

    def first_halving(pieces):
        products = jnp.stack(
            [jnp.dot(piece, down_weight, preferred_element_type=jnp.float32) for piece in pieces]
        )
        split = products.reshape(2, 2, half, products.shape[-1])
        keep = lax.dynamic_index_in_dim(split, low, 1, keepdims=False)
        send = lax.dynamic_index_in_dim(split, 1 - low, 1, keepdims=False)
        return keep + lax.ppermute(send, "tp", tp_pairs(1))

    def second_halving(summed):
        chosen = here % 2 ^ middle
        keep = lax.dynamic_index_in_dim(summed, chosen, 0, keepdims=False)
        send = lax.dynamic_index_in_dim(summed, 1 - chosen, 0, keepdims=False)
        return keep + lax.ppermute(send, "tp", tp_pairs(2))

    def first_halving_one(piece):
        product = jnp.dot(piece, down_weight, preferred_element_type=jnp.float32)
        split = product.reshape(2, half, product.shape[-1])
        keep = lax.dynamic_index_in_dim(split, low, 0, keepdims=False)
        send = lax.dynamic_index_in_dim(split, 1 - low, 0, keepdims=False)
        return keep + lax.ppermute(send, "tp", tp_pairs(1))

    near = second_halving(jnp.stack([first_halving_one(block), first_halving_one(across_x)]))
    far_summed = first_halving((across_y, diagonal))
    columns = near.shape[-1]
    width = columns // TAIL_PIECES
    chosen = here // 2 % 2 ^ high
    results = []
    previous = None
    for start in range(0, columns, width):
        piece = far_summed[..., start : start + width]
        if previous is not None:
            _, piece = lax.optimization_barrier((previous, piece))
        far = second_halving(piece)
        both = jnp.stack([near[:, start : start + width], far])
        keep = lax.dynamic_index_in_dim(both, chosen, 0, keepdims=False)
        send = lax.dynamic_index_in_dim(both, 1 - chosen, 0, keepdims=False)
        results.append(keep + lax.ppermute(send, "tp", tp_pairs(4)))
        previous = far
    return jnp.concatenate(results, axis=1)


def shards(hidden, down_weight, channel_scale):
    seq_count = lax.axis_size("seq")
    tp_count = lax.axis_size("tp")
    tokens, units = hidden.shape
    groups = tp_count // seq_count
    owned = tokens // groups
    piece = owned // CHUNKS
    grouped = hidden.reshape(groups, CHUNKS, piece, units)
    outputs = []
    for chunk in range(CHUNKS):
        part = grouped[:, chunk].reshape(groups * piece, units)
        if tp_count == 8:
            rotated = spread_rotate_return(part)
        else:
            spread = lax.all_to_all(part, "tp", split_axis=0, concat_axis=1, tiled=True)
            turned = rotate(spread)
            rotated = lax.all_to_all(turned, "tp", split_axis=1, concat_axis=0, tiled=True)
        if seq_count == 4 and tp_count == 8:
            outputs.append(product_and_reduce(rotated, down_weight))
        else:
            partial_terms = gathered_product(rotated, down_weight)
            outputs.append(scatter_sum_tp(partial_terms))
    summed = jnp.concatenate(outputs, axis=0)
    return (summed * channel_scale[None, :]).astype(jnp.bfloat16)


def solution(mesh):
    placed = (P("seq", "tp"), P("tp", "seq"), P("seq"))
    return jax.shard_map(
        shards, mesh=mesh, in_specs=placed, out_specs=P("tp", "seq"), check_vma=False
    )
```

```python
import math

import jax
import jax.numpy as jnp
import numpy as np
from jax import lax
from jax.sharding import PartitionSpec as P

PALEY = 28
INNER = 32
CHUNKS = 1
TAIL_PIECES = 4


def paley_table():
    residues = set((value * value % 13 for value in range(1, 13)))
    conference = np.zeros((14, 14))
    conference[0, 1:] = 1.0
    conference[1:, 0] = 1.0
    for first in range(13):
        for second in range(13):
            gap = (second - first) % 13
            if gap != 0:
                conference[1 + first, 1 + second] = 1.0 if gap in residues else -1.0
    upper = np.array([[1.0, 1.0], [1.0, -1.0]])
    lower = np.array([[1.0, -1.0], [-1.0, -1.0]])
    return np.kron(conference, upper) + np.kron(np.eye(14), lower)


def walsh_table(order):
    index_rows = np.arange(order)[:, None]
    index_cols = np.arange(order)[None, :]
    signs = np.ones((order, order))
    bit_value = 1
    while bit_value < order:
        both_set = index_rows // bit_value % 2 * (index_cols // bit_value % 2)
        signs = signs * (1 - 2 * both_set)
        bit_value = bit_value * 2
    return signs


def rotate(spread):
    rows, total_units = spread.shape
    walsh = total_units // PALEY
    outer_order = walsh // INNER
    width = INNER * PALEY
    inner_table = jnp.asarray(np.kron(walsh_table(INNER), paley_table()), jnp.bfloat16)
    outer_table = jnp.asarray(walsh_table(outer_order), jnp.float32)
    blocks = spread.reshape(rows, outer_order, width)
    inner = jnp.einsum("rbl,lm->rbm", blocks, inner_table, preferred_element_type=jnp.float32)
    outer = jnp.einsum("rbm,bc->rcm", inner, outer_table, precision=lax.Precision.HIGHEST)
    factor = 1.0 / math.sqrt(total_units)
    return (outer * factor).astype(jnp.bfloat16).reshape(rows, total_units)


def gathered_product(block, down_weight):
    seq_count = lax.axis_size("seq")
    if seq_count != 4:
        gathered = lax.all_gather(block, "seq", axis=0, tiled=True)
        return jnp.dot(gathered, down_weight, preferred_element_type=jnp.float32)
    rows = block.shape[0]
    half = rows // 2
    across_x = lax.ppermute(block, "seq", [(s, s ^ 1) for s in range(4)])
    across_y = lax.ppermute(block, "seq", [(s, s ^ 2) for s in range(4)])
    first = lax.ppermute(across_y[:half], "seq", [(s, s ^ 1) for s in range(4)])
    second = lax.ppermute(across_x[half:], "seq", [(s, s ^ 2) for s in range(4)])
    diagonal = jnp.concatenate([first, second], axis=0)
    me = lax.axis_index("seq")
    columns = down_weight.shape[1]
    result = jnp.zeros((4 * rows, columns), jnp.float32)
    for other, piece in enumerate((block, across_x, across_y, diagonal)):
        product = jnp.dot(piece, down_weight, preferred_element_type=jnp.float32)
        result = lax.dynamic_update_slice_in_dim(result, product, (me ^ other) * rows, 0)
    return result


def scatter_sum_tp(partial_terms):
    tp_count = lax.axis_size("tp")
    if tp_count != 8:
        return lax.psum_scatter(partial_terms, "tp", scatter_dimension=0, tiled=True)
    rows, columns = partial_terms.shape
    share = rows // tp_count
    me = lax.axis_index("tp")
    pairs = lambda distance: [(k, k ^ distance) for k in range(tp_count)]
    blocks = partial_terms.reshape(2, 2, 2, share, columns)
    low = me % 2
    keep = lax.dynamic_index_in_dim(blocks, low, 2, keepdims=False)
    send = lax.dynamic_index_in_dim(blocks, 1 - low, 2, keepdims=False)
    summed = keep + lax.ppermute(send, "tp", pairs(1))
    middle = me // 2 % 2
    keep = lax.dynamic_index_in_dim(summed, middle, 1, keepdims=False)
    send = lax.dynamic_index_in_dim(summed, 1 - middle, 1, keepdims=False)
    summed = keep + lax.ppermute(send, "tp", pairs(2))
    high = me // 4 % 2
    keep = lax.dynamic_index_in_dim(summed, high, 0, keepdims=False)
    send = lax.dynamic_index_in_dim(summed, 1 - high, 0, keepdims=False)
    return keep + lax.ppermute(send, "tp", pairs(4))


def spread_rotate_return(part):
    tp_count = lax.axis_size("tp")
    rows, units = part.shape
    share = rows // tp_count
    width = INNER * PALEY
    sub = units // width
    me = lax.axis_index("tp")
    pairs = lambda distance: [(k, k ^ distance) for k in range(tp_count)]
    inner_table = jnp.asarray(np.kron(walsh_table(INNER), paley_table()), jnp.bfloat16)
    landed = []
    for distance in range(tp_count):
        send = lax.dynamic_slice_in_dim(part, (me ^ distance) * share, share, 0)
        if distance:
            send = lax.ppermute(send, "tp", pairs(distance))
        landed.append(
            jnp.einsum(
                "rbl,lm->rbm",
                send.reshape(share, sub, width),
                inner_table,
                preferred_element_type=jnp.float32,
            )
        )
    inner = jnp.stack(landed, axis=1).reshape(share, tp_count * sub, width)
    order = jnp.arange(tp_count, dtype=jnp.int32)
    source = me ^ order
    signs = 1 - 2 * (lax.population_count(source[:, None] & source[None, :]) % 2)
    mixing = jnp.kron(signs.astype(jnp.float32), jnp.asarray(walsh_table(sub), jnp.float32))
    outer = jnp.einsum("rbm,bc->rcm", inner, mixing, precision=lax.Precision.HIGHEST)
    factor = 1.0 / math.sqrt(units * tp_count)
    turned = (outer * factor).astype(jnp.bfloat16).reshape(share, tp_count, units)
    result = jnp.zeros((rows, units), jnp.bfloat16)
    for distance in range(tp_count):
        block = turned[:, distance]
        if distance:
            block = lax.ppermute(block, "tp", pairs(distance))
        result = lax.dynamic_update_slice_in_dim(result, block, (me ^ distance) * share, 0)
    return result


def product_and_reduce(block, down_weight):
    rows = block.shape[0]
    half = rows // 2
    seq_pairs = lambda distance: [(s, s ^ distance) for s in range(4)]
    tp_pairs = lambda distance: [(k, k ^ distance) for k in range(8)]
    here = lax.axis_index("seq")
    me = lax.axis_index("tp")
    low, middle, high = me % 2, me // 2 % 2, me // 4 % 2
    across_x = lax.ppermute(block, "seq", seq_pairs(1))
    across_y = lax.ppermute(block, "seq", seq_pairs(2))
    first = lax.ppermute(across_y[:half], "seq", seq_pairs(1))
    second = lax.ppermute(across_x[half:], "seq", seq_pairs(2))
    diagonal = jnp.concatenate([first, second], axis=0)

    def first_halving(pieces):
        products = jnp.stack(
            [jnp.dot(piece, down_weight, preferred_element_type=jnp.float32) for piece in pieces]
        )
        split = products.reshape(2, 2, half, products.shape[-1])
        keep = lax.dynamic_index_in_dim(split, low, 1, keepdims=False)
        send = lax.dynamic_index_in_dim(split, 1 - low, 1, keepdims=False)
        return keep + lax.ppermute(send, "tp", tp_pairs(1))

    def second_halving(summed):
        chosen = here % 2 ^ middle
        keep = lax.dynamic_index_in_dim(summed, chosen, 0, keepdims=False)
        send = lax.dynamic_index_in_dim(summed, 1 - chosen, 0, keepdims=False)
        return keep + lax.ppermute(send, "tp", tp_pairs(2))

    def first_halving_one(piece):
        product = jnp.dot(piece, down_weight, preferred_element_type=jnp.float32)
        split = product.reshape(2, half, product.shape[-1])
        keep = lax.dynamic_index_in_dim(split, low, 0, keepdims=False)
        send = lax.dynamic_index_in_dim(split, 1 - low, 0, keepdims=False)
        return keep + lax.ppermute(send, "tp", tp_pairs(1))

    near = second_halving(jnp.stack([first_halving_one(block), first_halving_one(across_x)]))
    far_summed = jnp.stack([first_halving_one(across_y), first_halving_one(diagonal)])
    columns = near.shape[-1]
    width = columns // TAIL_PIECES
    chosen = here // 2 % 2 ^ high
    results = []
    previous = None
    for start in range(0, columns, width):
        piece = far_summed[..., start : start + width]
        if previous is not None:
            _, piece = lax.optimization_barrier((previous, piece))
        far = second_halving(piece)
        both = jnp.stack([near[:, start : start + width], far])
        keep = lax.dynamic_index_in_dim(both, chosen, 0, keepdims=False)
        send = lax.dynamic_index_in_dim(both, 1 - chosen, 0, keepdims=False)
        results.append(keep + lax.ppermute(send, "tp", tp_pairs(4)))
        previous = far
    return jnp.concatenate(results, axis=1)


def shards(hidden, down_weight, channel_scale):
    seq_count = lax.axis_size("seq")
    tp_count = lax.axis_size("tp")
    tokens, units = hidden.shape
    groups = tp_count // seq_count
    owned = tokens // groups
    piece = owned // CHUNKS
    grouped = hidden.reshape(groups, CHUNKS, piece, units)
    outputs = []
    for chunk in range(CHUNKS):
        part = grouped[:, chunk].reshape(groups * piece, units)
        if tp_count == 8:
            rotated = spread_rotate_return(part)
        else:
            spread = lax.all_to_all(part, "tp", split_axis=0, concat_axis=1, tiled=True)
            turned = rotate(spread)
            rotated = lax.all_to_all(turned, "tp", split_axis=1, concat_axis=0, tiled=True)
        if seq_count == 4 and tp_count == 8:
            outputs.append(product_and_reduce(rotated, down_weight))
        else:
            partial_terms = gathered_product(rotated, down_weight)
            outputs.append(scatter_sum_tp(partial_terms))
    summed = jnp.concatenate(outputs, axis=0)
    return (summed * channel_scale[None, :]).astype(jnp.bfloat16)


def solution(mesh):
    placed = (P("seq", "tp"), P("tp", "seq"), P("seq"))
    return jax.shard_map(
        shards, mesh=mesh, in_specs=placed, out_specs=P("tp", "seq"), check_vma=False
    )
```

```python
import math

import jax
import jax.numpy as jnp
import numpy as np
from jax import lax
from jax.sharding import PartitionSpec as P

PALEY = 28
INNER = 32
CHUNKS = 1
TAIL_PIECES = 2


def paley_table():
    residues = set((value * value % 13 for value in range(1, 13)))
    conference = np.zeros((14, 14))
    conference[0, 1:] = 1.0
    conference[1:, 0] = 1.0
    for first in range(13):
        for second in range(13):
            gap = (second - first) % 13
            if gap != 0:
                conference[1 + first, 1 + second] = 1.0 if gap in residues else -1.0
    upper = np.array([[1.0, 1.0], [1.0, -1.0]])
    lower = np.array([[1.0, -1.0], [-1.0, -1.0]])
    return np.kron(conference, upper) + np.kron(np.eye(14), lower)


def walsh_table(order):
    index_rows = np.arange(order)[:, None]
    index_cols = np.arange(order)[None, :]
    signs = np.ones((order, order))
    bit_value = 1
    while bit_value < order:
        both_set = index_rows // bit_value % 2 * (index_cols // bit_value % 2)
        signs = signs * (1 - 2 * both_set)
        bit_value = bit_value * 2
    return signs


def rotate(spread):
    rows, total_units = spread.shape
    walsh = total_units // PALEY
    outer_order = walsh // INNER
    width = INNER * PALEY
    inner_table = jnp.asarray(np.kron(walsh_table(INNER), paley_table()), jnp.bfloat16)
    outer_table = jnp.asarray(walsh_table(outer_order), jnp.float32)
    blocks = spread.reshape(rows, outer_order, width)
    inner = jnp.einsum("rbl,lm->rbm", blocks, inner_table, preferred_element_type=jnp.float32)
    outer = jnp.einsum("rbm,bc->rcm", inner, outer_table, precision=lax.Precision.HIGHEST)
    factor = 1.0 / math.sqrt(total_units)
    return (outer * factor).astype(jnp.bfloat16).reshape(rows, total_units)


def gathered_product(block, down_weight):
    seq_count = lax.axis_size("seq")
    if seq_count != 4:
        gathered = lax.all_gather(block, "seq", axis=0, tiled=True)
        return jnp.dot(gathered, down_weight, preferred_element_type=jnp.float32)
    rows = block.shape[0]
    half = rows // 2
    across_x = lax.ppermute(block, "seq", [(s, s ^ 1) for s in range(4)])
    across_y = lax.ppermute(block, "seq", [(s, s ^ 2) for s in range(4)])
    first = lax.ppermute(across_y[:half], "seq", [(s, s ^ 1) for s in range(4)])
    second = lax.ppermute(across_x[half:], "seq", [(s, s ^ 2) for s in range(4)])
    diagonal = jnp.concatenate([first, second], axis=0)
    me = lax.axis_index("seq")
    columns = down_weight.shape[1]
    result = jnp.zeros((4 * rows, columns), jnp.float32)
    for other, piece in enumerate((block, across_x, across_y, diagonal)):
        product = jnp.dot(piece, down_weight, preferred_element_type=jnp.float32)
        result = lax.dynamic_update_slice_in_dim(result, product, (me ^ other) * rows, 0)
    return result


def scatter_sum_tp(partial_terms):
    tp_count = lax.axis_size("tp")
    if tp_count != 8:
        return lax.psum_scatter(partial_terms, "tp", scatter_dimension=0, tiled=True)
    rows, columns = partial_terms.shape
    share = rows // tp_count
    me = lax.axis_index("tp")
    pairs = lambda distance: [(k, k ^ distance) for k in range(tp_count)]
    blocks = partial_terms.reshape(2, 2, 2, share, columns)
    low = me % 2
    keep = lax.dynamic_index_in_dim(blocks, low, 2, keepdims=False)
    send = lax.dynamic_index_in_dim(blocks, 1 - low, 2, keepdims=False)
    summed = keep + lax.ppermute(send, "tp", pairs(1))
    middle = me // 2 % 2
    keep = lax.dynamic_index_in_dim(summed, middle, 1, keepdims=False)
    send = lax.dynamic_index_in_dim(summed, 1 - middle, 1, keepdims=False)
    summed = keep + lax.ppermute(send, "tp", pairs(2))
    high = me // 4 % 2
    keep = lax.dynamic_index_in_dim(summed, high, 0, keepdims=False)
    send = lax.dynamic_index_in_dim(summed, 1 - high, 0, keepdims=False)
    return keep + lax.ppermute(send, "tp", pairs(4))


def spread_rotate_return(part):
    tp_count = lax.axis_size("tp")
    rows, units = part.shape
    share = rows // tp_count
    width = INNER * PALEY
    sub = units // width
    me = lax.axis_index("tp")
    pairs = lambda distance: [(k, k ^ distance) for k in range(tp_count)]
    inner_table = jnp.asarray(np.kron(walsh_table(INNER), paley_table()), jnp.bfloat16)
    landed = []
    for distance in range(tp_count):
        send = lax.dynamic_slice_in_dim(part, (me ^ distance) * share, share, 0)
        if distance:
            send = lax.ppermute(send, "tp", pairs(distance))
        landed.append(
            jnp.einsum(
                "rbl,lm->rbm",
                send.reshape(share, sub, width),
                inner_table,
                preferred_element_type=jnp.float32,
            )
        )
    inner = jnp.stack(landed, axis=1).reshape(share, tp_count * sub, width)
    order = jnp.arange(tp_count, dtype=jnp.int32)
    source = me ^ order
    signs = 1 - 2 * (lax.population_count(source[:, None] & source[None, :]) % 2)
    mixing = jnp.kron(signs.astype(jnp.float32), jnp.asarray(walsh_table(sub), jnp.float32))
    outer = jnp.einsum("rbm,bc->rcm", inner, mixing, precision=lax.Precision.HIGHEST)
    factor = 1.0 / math.sqrt(units * tp_count)
    turned = (outer * factor).astype(jnp.bfloat16).reshape(share, tp_count, units)
    result = jnp.zeros((rows, units), jnp.bfloat16)
    for distance in range(tp_count):
        block = turned[:, distance]
        if distance:
            block = lax.ppermute(block, "tp", pairs(distance))
        result = lax.dynamic_update_slice_in_dim(result, block, (me ^ distance) * share, 0)
    return result


def product_and_reduce(block, down_weight):
    rows = block.shape[0]
    half = rows // 2
    seq_pairs = lambda distance: [(s, s ^ distance) for s in range(4)]
    tp_pairs = lambda distance: [(k, k ^ distance) for k in range(8)]
    here = lax.axis_index("seq")
    me = lax.axis_index("tp")
    low, middle, high = me % 2, me // 2 % 2, me // 4 % 2
    across_x = lax.ppermute(block, "seq", seq_pairs(1))
    across_y = lax.ppermute(block, "seq", seq_pairs(2))
    first = lax.ppermute(across_y[:half], "seq", seq_pairs(1))
    second = lax.ppermute(across_x[half:], "seq", seq_pairs(2))
    diagonal = jnp.concatenate([first, second], axis=0)

    def first_halving(pieces):
        products = jnp.stack(
            [jnp.dot(piece, down_weight, preferred_element_type=jnp.float32) for piece in pieces]
        )
        split = products.reshape(2, 2, half, products.shape[-1])
        keep = lax.dynamic_index_in_dim(split, low, 1, keepdims=False)
        send = lax.dynamic_index_in_dim(split, 1 - low, 1, keepdims=False)
        return keep + lax.ppermute(send, "tp", tp_pairs(1))

    def second_halving(summed):
        chosen = here % 2 ^ middle
        keep = lax.dynamic_index_in_dim(summed, chosen, 0, keepdims=False)
        send = lax.dynamic_index_in_dim(summed, 1 - chosen, 0, keepdims=False)
        return keep + lax.ppermute(send, "tp", tp_pairs(2))

    def first_halving_one(piece):
        product = jnp.dot(piece, down_weight, preferred_element_type=jnp.float32)
        split = product.reshape(2, half, product.shape[-1])
        keep = lax.dynamic_index_in_dim(split, low, 0, keepdims=False)
        send = lax.dynamic_index_in_dim(split, 1 - low, 0, keepdims=False)
        return keep + lax.ppermute(send, "tp", tp_pairs(1))

    near = second_halving(jnp.stack([first_halving_one(block), first_halving_one(across_x)]))
    far_summed = first_halving((across_y, diagonal))
    columns = near.shape[-1]
    width = columns // TAIL_PIECES
    chosen = here // 2 % 2 ^ high
    results = []
    previous = None
    for start in range(0, columns, width):
        piece = far_summed[..., start : start + width]
        if previous is not None:
            _, piece = lax.optimization_barrier((previous, piece))
        far = second_halving(piece)
        both = jnp.stack([near[:, start : start + width], far])
        keep = lax.dynamic_index_in_dim(both, chosen, 0, keepdims=False)
        send = lax.dynamic_index_in_dim(both, 1 - chosen, 0, keepdims=False)
        results.append(keep + lax.ppermute(send, "tp", tp_pairs(4)))
        previous = far
    return jnp.concatenate(results, axis=1)


def shards(hidden, down_weight, channel_scale):
    seq_count = lax.axis_size("seq")
    tp_count = lax.axis_size("tp")
    tokens, units = hidden.shape
    groups = tp_count // seq_count
    owned = tokens // groups
    piece = owned // CHUNKS
    grouped = hidden.reshape(groups, CHUNKS, piece, units)
    outputs = []
    for chunk in range(CHUNKS):
        part = grouped[:, chunk].reshape(groups * piece, units)
        if tp_count == 8:
            rotated = spread_rotate_return(part)
        else:
            spread = lax.all_to_all(part, "tp", split_axis=0, concat_axis=1, tiled=True)
            turned = rotate(spread)
            rotated = lax.all_to_all(turned, "tp", split_axis=1, concat_axis=0, tiled=True)
        if seq_count == 4 and tp_count == 8:
            outputs.append(product_and_reduce(rotated, down_weight))
        else:
            partial_terms = gathered_product(rotated, down_weight)
            outputs.append(scatter_sum_tp(partial_terms))
    summed = jnp.concatenate(outputs, axis=0)
    return (summed * channel_scale[None, :]).astype(jnp.bfloat16)


def solution(mesh):
    placed = (P("seq", "tp"), P("tp", "seq"), P("seq"))
    return jax.shard_map(
        shards, mesh=mesh, in_specs=placed, out_specs=P("tp", "seq"), check_vma=False
    )
```

```python
import math

import jax
import jax.numpy as jnp
import numpy as np
from jax import lax
from jax.sharding import PartitionSpec as P

PALEY = 28
INNER = 32
CHUNKS = 1
TAIL_PIECES = 8


def paley_table():
    residues = set((value * value % 13 for value in range(1, 13)))
    conference = np.zeros((14, 14))
    conference[0, 1:] = 1.0
    conference[1:, 0] = 1.0
    for first in range(13):
        for second in range(13):
            gap = (second - first) % 13
            if gap != 0:
                conference[1 + first, 1 + second] = 1.0 if gap in residues else -1.0
    upper = np.array([[1.0, 1.0], [1.0, -1.0]])
    lower = np.array([[1.0, -1.0], [-1.0, -1.0]])
    return np.kron(conference, upper) + np.kron(np.eye(14), lower)


def walsh_table(order):
    index_rows = np.arange(order)[:, None]
    index_cols = np.arange(order)[None, :]
    signs = np.ones((order, order))
    bit_value = 1
    while bit_value < order:
        both_set = index_rows // bit_value % 2 * (index_cols // bit_value % 2)
        signs = signs * (1 - 2 * both_set)
        bit_value = bit_value * 2
    return signs


def rotate(spread):
    rows, total_units = spread.shape
    walsh = total_units // PALEY
    outer_order = walsh // INNER
    width = INNER * PALEY
    inner_table = jnp.asarray(np.kron(walsh_table(INNER), paley_table()), jnp.bfloat16)
    outer_table = jnp.asarray(walsh_table(outer_order), jnp.float32)
    blocks = spread.reshape(rows, outer_order, width)
    inner = jnp.einsum("rbl,lm->rbm", blocks, inner_table, preferred_element_type=jnp.float32)
    outer = jnp.einsum("rbm,bc->rcm", inner, outer_table, precision=lax.Precision.HIGHEST)
    factor = 1.0 / math.sqrt(total_units)
    return (outer * factor).astype(jnp.bfloat16).reshape(rows, total_units)


def gathered_product(block, down_weight):
    seq_count = lax.axis_size("seq")
    if seq_count != 4:
        gathered = lax.all_gather(block, "seq", axis=0, tiled=True)
        return jnp.dot(gathered, down_weight, preferred_element_type=jnp.float32)
    rows = block.shape[0]
    half = rows // 2
    across_x = lax.ppermute(block, "seq", [(s, s ^ 1) for s in range(4)])
    across_y = lax.ppermute(block, "seq", [(s, s ^ 2) for s in range(4)])
    first = lax.ppermute(across_y[:half], "seq", [(s, s ^ 1) for s in range(4)])
    second = lax.ppermute(across_x[half:], "seq", [(s, s ^ 2) for s in range(4)])
    diagonal = jnp.concatenate([first, second], axis=0)
    me = lax.axis_index("seq")
    columns = down_weight.shape[1]
    result = jnp.zeros((4 * rows, columns), jnp.float32)
    for other, piece in enumerate((block, across_x, across_y, diagonal)):
        product = jnp.dot(piece, down_weight, preferred_element_type=jnp.float32)
        result = lax.dynamic_update_slice_in_dim(result, product, (me ^ other) * rows, 0)
    return result


def scatter_sum_tp(partial_terms):
    tp_count = lax.axis_size("tp")
    if tp_count != 8:
        return lax.psum_scatter(partial_terms, "tp", scatter_dimension=0, tiled=True)
    rows, columns = partial_terms.shape
    share = rows // tp_count
    me = lax.axis_index("tp")
    pairs = lambda distance: [(k, k ^ distance) for k in range(tp_count)]
    blocks = partial_terms.reshape(2, 2, 2, share, columns)
    low = me % 2
    keep = lax.dynamic_index_in_dim(blocks, low, 2, keepdims=False)
    send = lax.dynamic_index_in_dim(blocks, 1 - low, 2, keepdims=False)
    summed = keep + lax.ppermute(send, "tp", pairs(1))
    middle = me // 2 % 2
    keep = lax.dynamic_index_in_dim(summed, middle, 1, keepdims=False)
    send = lax.dynamic_index_in_dim(summed, 1 - middle, 1, keepdims=False)
    summed = keep + lax.ppermute(send, "tp", pairs(2))
    high = me // 4 % 2
    keep = lax.dynamic_index_in_dim(summed, high, 0, keepdims=False)
    send = lax.dynamic_index_in_dim(summed, 1 - high, 0, keepdims=False)
    return keep + lax.ppermute(send, "tp", pairs(4))


def spread_rotate_return(part):
    tp_count = lax.axis_size("tp")
    rows, units = part.shape
    share = rows // tp_count
    width = INNER * PALEY
    sub = units // width
    me = lax.axis_index("tp")
    pairs = lambda distance: [(k, k ^ distance) for k in range(tp_count)]
    inner_table = jnp.asarray(np.kron(walsh_table(INNER), paley_table()), jnp.bfloat16)
    landed = []
    for distance in range(tp_count):
        send = lax.dynamic_slice_in_dim(part, (me ^ distance) * share, share, 0)
        if distance:
            send = lax.ppermute(send, "tp", pairs(distance))
        landed.append(
            jnp.einsum(
                "rbl,lm->rbm",
                send.reshape(share, sub, width),
                inner_table,
                preferred_element_type=jnp.float32,
            )
        )
    inner = jnp.stack(landed, axis=1).reshape(share, tp_count * sub, width)
    order = jnp.arange(tp_count, dtype=jnp.int32)
    source = me ^ order
    signs = 1 - 2 * (lax.population_count(source[:, None] & source[None, :]) % 2)
    mixing = jnp.kron(signs.astype(jnp.float32), jnp.asarray(walsh_table(sub), jnp.float32))
    outer = jnp.einsum("rbm,bc->rcm", inner, mixing, precision=lax.Precision.HIGHEST)
    factor = 1.0 / math.sqrt(units * tp_count)
    turned = (outer * factor).astype(jnp.bfloat16).reshape(share, tp_count, units)
    result = jnp.zeros((rows, units), jnp.bfloat16)
    for distance in range(tp_count):
        block = turned[:, distance]
        if distance:
            block = lax.ppermute(block, "tp", pairs(distance))
        result = lax.dynamic_update_slice_in_dim(result, block, (me ^ distance) * share, 0)
    return result


def product_and_reduce(block, down_weight):
    rows = block.shape[0]
    half = rows // 2
    seq_pairs = lambda distance: [(s, s ^ distance) for s in range(4)]
    tp_pairs = lambda distance: [(k, k ^ distance) for k in range(8)]
    here = lax.axis_index("seq")
    me = lax.axis_index("tp")
    low, middle, high = me % 2, me // 2 % 2, me // 4 % 2
    across_x = lax.ppermute(block, "seq", seq_pairs(1))
    across_y = lax.ppermute(block, "seq", seq_pairs(2))
    first = lax.ppermute(across_y[:half], "seq", seq_pairs(1))
    second = lax.ppermute(across_x[half:], "seq", seq_pairs(2))
    diagonal = jnp.concatenate([first, second], axis=0)

    def first_halving(pieces):
        products = jnp.stack(
            [jnp.dot(piece, down_weight, preferred_element_type=jnp.float32) for piece in pieces]
        )
        split = products.reshape(2, 2, half, products.shape[-1])
        keep = lax.dynamic_index_in_dim(split, low, 1, keepdims=False)
        send = lax.dynamic_index_in_dim(split, 1 - low, 1, keepdims=False)
        return keep + lax.ppermute(send, "tp", tp_pairs(1))

    def second_halving(summed):
        chosen = here % 2 ^ middle
        keep = lax.dynamic_index_in_dim(summed, chosen, 0, keepdims=False)
        send = lax.dynamic_index_in_dim(summed, 1 - chosen, 0, keepdims=False)
        return keep + lax.ppermute(send, "tp", tp_pairs(2))

    def first_halving_one(piece):
        product = jnp.dot(piece, down_weight, preferred_element_type=jnp.float32)
        split = product.reshape(2, half, product.shape[-1])
        keep = lax.dynamic_index_in_dim(split, low, 0, keepdims=False)
        send = lax.dynamic_index_in_dim(split, 1 - low, 0, keepdims=False)
        return keep + lax.ppermute(send, "tp", tp_pairs(1))

    near = second_halving(jnp.stack([first_halving_one(block), first_halving_one(across_x)]))
    far_summed = first_halving((across_y, diagonal))
    columns = near.shape[-1]
    width = columns // TAIL_PIECES
    chosen = here // 2 % 2 ^ high
    results = []
    previous = None
    for start in range(0, columns, width):
        piece = far_summed[..., start : start + width]
        if previous is not None:
            _, piece = lax.optimization_barrier((previous, piece))
        far = second_halving(piece)
        both = jnp.stack([near[:, start : start + width], far])
        keep = lax.dynamic_index_in_dim(both, chosen, 0, keepdims=False)
        send = lax.dynamic_index_in_dim(both, 1 - chosen, 0, keepdims=False)
        results.append(keep + lax.ppermute(send, "tp", tp_pairs(4)))
        previous = far
    return jnp.concatenate(results, axis=1)


def shards(hidden, down_weight, channel_scale):
    seq_count = lax.axis_size("seq")
    tp_count = lax.axis_size("tp")
    tokens, units = hidden.shape
    groups = tp_count // seq_count
    owned = tokens // groups
    piece = owned // CHUNKS
    grouped = hidden.reshape(groups, CHUNKS, piece, units)
    outputs = []
    for chunk in range(CHUNKS):
        part = grouped[:, chunk].reshape(groups * piece, units)
        if tp_count == 8:
            rotated = spread_rotate_return(part)
        else:
            spread = lax.all_to_all(part, "tp", split_axis=0, concat_axis=1, tiled=True)
            turned = rotate(spread)
            rotated = lax.all_to_all(turned, "tp", split_axis=1, concat_axis=0, tiled=True)
        if seq_count == 4 and tp_count == 8:
            outputs.append(product_and_reduce(rotated, down_weight))
        else:
            partial_terms = gathered_product(rotated, down_weight)
            outputs.append(scatter_sum_tp(partial_terms))
    summed = jnp.concatenate(outputs, axis=0)
    return (summed * channel_scale[None, :]).astype(jnp.bfloat16)


def solution(mesh):
    placed = (P("seq", "tp"), P("tp", "seq"), P("seq"))
    return jax.shard_map(
        shards, mesh=mesh, in_specs=placed, out_specs=P("tp", "seq"), check_vma=False
    )
```

```python
import math

import jax
import jax.numpy as jnp
import numpy as np
from jax import lax
from jax.sharding import PartitionSpec as P

PALEY = 28
INNER = 32
CHUNKS = 1
TAIL_PIECES = 4


def paley_table():
    residues = set((value * value % 13 for value in range(1, 13)))
    conference = np.zeros((14, 14))
    conference[0, 1:] = 1.0
    conference[1:, 0] = 1.0
    for first in range(13):
        for second in range(13):
            gap = (second - first) % 13
            if gap != 0:
                conference[1 + first, 1 + second] = 1.0 if gap in residues else -1.0
    upper = np.array([[1.0, 1.0], [1.0, -1.0]])
    lower = np.array([[1.0, -1.0], [-1.0, -1.0]])
    return np.kron(conference, upper) + np.kron(np.eye(14), lower)


def walsh_table(order):
    index_rows = np.arange(order)[:, None]
    index_cols = np.arange(order)[None, :]
    signs = np.ones((order, order))
    bit_value = 1
    while bit_value < order:
        both_set = index_rows // bit_value % 2 * (index_cols // bit_value % 2)
        signs = signs * (1 - 2 * both_set)
        bit_value = bit_value * 2
    return signs


def rotate(spread):
    rows, total_units = spread.shape
    walsh = total_units // PALEY
    outer_order = walsh // INNER
    width = INNER * PALEY
    inner_table = jnp.asarray(np.kron(walsh_table(INNER), paley_table()), jnp.bfloat16)
    outer_table = jnp.asarray(walsh_table(outer_order), jnp.float32)
    blocks = spread.reshape(rows, outer_order, width)
    inner = jnp.einsum("rbl,lm->rbm", blocks, inner_table, preferred_element_type=jnp.float32)
    outer = jnp.einsum("rbm,bc->rcm", inner, outer_table, precision=lax.Precision.HIGHEST)
    factor = 1.0 / math.sqrt(total_units)
    return (outer * factor).astype(jnp.bfloat16).reshape(rows, total_units)


def gathered_product(block, down_weight):
    seq_count = lax.axis_size("seq")
    if seq_count != 4:
        gathered = lax.all_gather(block, "seq", axis=0, tiled=True)
        return jnp.dot(gathered, down_weight, preferred_element_type=jnp.float32)
    rows = block.shape[0]
    half = rows // 2
    across_x = lax.ppermute(block, "seq", [(s, s ^ 1) for s in range(4)])
    across_y = lax.ppermute(block, "seq", [(s, s ^ 2) for s in range(4)])
    first = lax.ppermute(across_y[:half], "seq", [(s, s ^ 1) for s in range(4)])
    second = lax.ppermute(across_x[half:], "seq", [(s, s ^ 2) for s in range(4)])
    diagonal = jnp.concatenate([first, second], axis=0)
    me = lax.axis_index("seq")
    columns = down_weight.shape[1]
    result = jnp.zeros((4 * rows, columns), jnp.float32)
    for other, piece in enumerate((block, across_x, across_y, diagonal)):
        product = jnp.dot(piece, down_weight, preferred_element_type=jnp.float32)
        result = lax.dynamic_update_slice_in_dim(result, product, (me ^ other) * rows, 0)
    return result


def scatter_sum_tp(partial_terms):
    tp_count = lax.axis_size("tp")
    if tp_count != 8:
        return lax.psum_scatter(partial_terms, "tp", scatter_dimension=0, tiled=True)
    rows, columns = partial_terms.shape
    share = rows // tp_count
    me = lax.axis_index("tp")
    pairs = lambda distance: [(k, k ^ distance) for k in range(tp_count)]
    blocks = partial_terms.reshape(2, 2, 2, share, columns)
    low = me % 2
    keep = lax.dynamic_index_in_dim(blocks, low, 2, keepdims=False)
    send = lax.dynamic_index_in_dim(blocks, 1 - low, 2, keepdims=False)
    summed = keep + lax.ppermute(send, "tp", pairs(1))
    middle = me // 2 % 2
    keep = lax.dynamic_index_in_dim(summed, middle, 1, keepdims=False)
    send = lax.dynamic_index_in_dim(summed, 1 - middle, 1, keepdims=False)
    summed = keep + lax.ppermute(send, "tp", pairs(2))
    high = me // 4 % 2
    keep = lax.dynamic_index_in_dim(summed, high, 0, keepdims=False)
    send = lax.dynamic_index_in_dim(summed, 1 - high, 0, keepdims=False)
    return keep + lax.ppermute(send, "tp", pairs(4))


def spread_rotate_return(part):
    tp_count = lax.axis_size("tp")
    rows, units = part.shape
    share = rows // tp_count
    width = INNER * PALEY
    sub = units // width
    me = lax.axis_index("tp")
    pairs = lambda distance: [(k, k ^ distance) for k in range(tp_count)]
    inner_table = jnp.asarray(np.kron(walsh_table(INNER), paley_table()), jnp.bfloat16)
    landed = []
    for distance in range(tp_count):
        send = lax.dynamic_slice_in_dim(part, (me ^ distance) * share, share, 0)
        if distance:
            send = lax.ppermute(send, "tp", pairs(distance))
        landed.append(
            jnp.einsum(
                "rbl,lm->rbm",
                send.reshape(share, sub, width),
                inner_table,
                preferred_element_type=jnp.float32,
            )
        )
    inner = jnp.stack(landed, axis=1).reshape(share, tp_count * sub, width)
    order = jnp.arange(tp_count, dtype=jnp.int32)
    source = me ^ order
    signs = 1 - 2 * (lax.population_count(source[:, None] & source[None, :]) % 2)
    mixing = jnp.kron(signs.astype(jnp.float32), jnp.asarray(walsh_table(sub), jnp.float32))
    outer = jnp.einsum("rbm,bc->rcm", inner, mixing, precision=lax.Precision.HIGHEST)
    factor = 1.0 / math.sqrt(units * tp_count)
    turned = (outer * factor).astype(jnp.bfloat16).reshape(share, tp_count, units)
    result = jnp.zeros((rows, units), jnp.bfloat16)
    for distance in range(tp_count):
        block = turned[:, distance]
        if distance:
            block = lax.ppermute(block, "tp", pairs(distance))
        result = lax.dynamic_update_slice_in_dim(result, block, (me ^ distance) * share, 0)
    return result


def product_and_reduce(block, down_weight):
    rows = block.shape[0]
    half = rows // 2
    seq_pairs = lambda distance: [(s, s ^ distance) for s in range(4)]
    tp_pairs = lambda distance: [(k, k ^ distance) for k in range(8)]
    here = lax.axis_index("seq")
    me = lax.axis_index("tp")
    low, middle, high = me % 2, me // 2 % 2, me // 4 % 2
    across_x = lax.ppermute(block, "seq", seq_pairs(1))
    across_y = lax.ppermute(block, "seq", seq_pairs(2))
    first = lax.ppermute(across_y[:half], "seq", seq_pairs(1))
    second = lax.ppermute(across_x[half:], "seq", seq_pairs(2))
    diagonal = jnp.concatenate([first, second], axis=0)

    def first_halving(pieces):
        products = jnp.stack(
            [jnp.dot(piece, down_weight, preferred_element_type=jnp.float32) for piece in pieces]
        )
        split = products.reshape(2, 2, half, products.shape[-1])
        keep = lax.dynamic_index_in_dim(split, low, 1, keepdims=False)
        send = lax.dynamic_index_in_dim(split, 1 - low, 1, keepdims=False)
        return keep + lax.ppermute(send, "tp", tp_pairs(1))

    def second_halving(summed):
        chosen = here % 2 ^ middle
        keep = lax.dynamic_index_in_dim(summed, chosen, 0, keepdims=False)
        send = lax.dynamic_index_in_dim(summed, 1 - chosen, 0, keepdims=False)
        return keep + lax.ppermute(send, "tp", tp_pairs(2))

    def first_halving_one(piece):
        product = jnp.dot(piece, down_weight, preferred_element_type=jnp.float32)
        split = product.reshape(2, half, product.shape[-1])
        keep = lax.dynamic_index_in_dim(split, low, 0, keepdims=False)
        send = lax.dynamic_index_in_dim(split, 1 - low, 0, keepdims=False)
        return keep + lax.ppermute(send, "tp", tp_pairs(1))

    near_summed = jnp.stack([first_halving_one(block), first_halving_one(across_x)])
    near_width = near_summed.shape[-1] // 2
    near = jnp.concatenate(
        [
            second_halving(near_summed[..., start : start + near_width])
            for start in (0, near_width)
        ],
        axis=1,
    )
    far_summed = first_halving((across_y, diagonal))
    columns = near.shape[-1]
    width = columns // TAIL_PIECES
    chosen = here // 2 % 2 ^ high
    results = []
    previous = None
    for start in range(0, columns, width):
        piece = far_summed[..., start : start + width]
        if previous is not None:
            _, piece = lax.optimization_barrier((previous, piece))
        far = second_halving(piece)
        both = jnp.stack([near[:, start : start + width], far])
        keep = lax.dynamic_index_in_dim(both, chosen, 0, keepdims=False)
        send = lax.dynamic_index_in_dim(both, 1 - chosen, 0, keepdims=False)
        results.append(keep + lax.ppermute(send, "tp", tp_pairs(4)))
        previous = far
    return jnp.concatenate(results, axis=1)


def shards(hidden, down_weight, channel_scale):
    seq_count = lax.axis_size("seq")
    tp_count = lax.axis_size("tp")
    tokens, units = hidden.shape
    groups = tp_count // seq_count
    owned = tokens // groups
    piece = owned // CHUNKS
    grouped = hidden.reshape(groups, CHUNKS, piece, units)
    outputs = []
    for chunk in range(CHUNKS):
        part = grouped[:, chunk].reshape(groups * piece, units)
        if tp_count == 8:
            rotated = spread_rotate_return(part)
        else:
            spread = lax.all_to_all(part, "tp", split_axis=0, concat_axis=1, tiled=True)
            turned = rotate(spread)
            rotated = lax.all_to_all(turned, "tp", split_axis=1, concat_axis=0, tiled=True)
        if seq_count == 4 and tp_count == 8:
            outputs.append(product_and_reduce(rotated, down_weight))
        else:
            partial_terms = gathered_product(rotated, down_weight)
            outputs.append(scatter_sum_tp(partial_terms))
    summed = jnp.concatenate(outputs, axis=0)
    return (summed * channel_scale[None, :]).astype(jnp.bfloat16)


def solution(mesh):
    placed = (P("seq", "tp"), P("tp", "seq"), P("seq"))
    return jax.shard_map(
        shards, mesh=mesh, in_specs=placed, out_specs=P("tp", "seq"), check_vma=False
    )
```
